256 devices in a mesh: ctx: 16 (over y_lo, z), exp: 8 (over x, core), rep: 2 (over y_hi).
Axes of the slice: x: 4, y: 4 (y_hi: 2, y_lo: 2; y = y_hi * 2 + y_lo), z: 8, core: 2. Of those that a mesh axis runs over, the one named last changes fastest.
Arguments:
- sequence: bfloat16 [2, 2048, 2048], P('rep', 'ctx'), may hold values from -6 to 6
- norm1_gain: float32 [2048], replicated, may hold values from 0.1 to 1.9
- w_in: bfloat16 [2048, 3, 2048], P(None, None, 'exp'), may hold values from -0.125 to 0.125
- long_filter: float32 [2048, 2048], P('ctx', 'exp'), may hold values from -0.125 to 0.125
- filter_decay: float32 [2048], P('exp'), may hold values from 0.5 to 150
- conv_bias: float32 [2048], P('exp'), may hold values from -4 to 4
- w_out: bfloat16 [2048, 2048], P('exp'), may hold values from -0.125 to 0.125
- norm2_gain: float32 [2048], replicated, may hold values from 0.1 to 1.9
- router: bfloat16 [2048, 8], replicated, may hold values from -0.39648438 to 0.39648438
- w_gate: bfloat16 [8, 2048, 4096], P('exp', None, 'ctx'), may hold values from -0.125 to 0.125
- w_up: bfloat16 [8, 2048, 4096], P('exp', None, 'ctx'), may hold values from -0.125 to 0.125
- w_down: bfloat16 [8, 4096, 2048], P('exp', 'ctx'), may hold values from -0.09375 to 0.09375
- experts: int32 [2, 2048, 2], P('rep', ('ctx', 'exp')), may hold values from 0 to 7, as said below
- expert_slots: int32 [2, 2048, 2], P('rep', ('ctx', 'exp')), may hold values from 0 to 7, as said below
- splice_head: bfloat16 [112, 2048], replicated, may hold values from -0.125 to 0.125
- targets: float32 [2, 2048, 112], P('rep', ('ctx', 'exp')), may hold values from 0 to 1
Outputs:
- block_out: bfloat16 [2, 2048, 2048], P('rep', ('ctx', 'exp'))
- head_grad: float32 [112, 2048], replicated
The draws below stay inside these ranges and needn't reach their ends.
Inputs may be any that keep to these rules, and one draw needn't show every extreme that they name: Each token names two different experts. Among the tokens of one aligned block of 16 tokens, no expert is named more than 8 times, and in each replica one expert is named exactly 8 times in every block. `expert_slots`: A choice's slot is the number of choices of the same expert before it within its aligned block of 16 tokens, in token order, a token's first choice before its second.
All inputs are finite; a program needn't handle non-finite values.
Results may differ from the reference program's by a relative error of at most 0.011.
Values may be sent and summed in bfloat16 or wider, within the bound.
No kernel may reach another device: no remote copies, remote signals or barrier semaphores. Data moves between devices by JAX's collectives and lax.ppermute only.
A program may use at most 64 MiB of HBM per device.

```python
import math
import jax
import jax.numpy as jnp
from jax import lax

D = 2048
HIDDEN_SIZE = 4096
TOK_DEV = 16
LENGTH = 2048
REPS = 2
EXPERTS = 8
CAP = 8
HID_DEV = 256
HEAD_OUT = 112
N_CTX = 16


def routing_tables(key):
    block_count = LENGTH // TOK_DEV

    def one_block(block_key, full_id):
        key_perm, key_order, key_flip = jax.random.split(block_key, 3)
        seats = jnp.arange((EXPERTS - 1) * CAP, dtype=jnp.int32) // CAP
        seats = seats + (seats >= full_id).astype(jnp.int32)
        taken = jax.random.permutation(key_perm, seats)[:2 * TOK_DEV - CAP]
        ordered = jnp.sort(jnp.concatenate([jnp.full((CAP,), full_id, jnp.int32), taken]))
        paired = jnp.stack([ordered[:TOK_DEV], ordered[TOK_DEV:]], axis=1)
        paired = paired[jax.random.permutation(key_order, TOK_DEV)]
        flips = jax.random.randint(key_flip, (TOK_DEV, 1), 0, 2)
        paired = jnp.where(flips == 1, paired[:, ::-1], paired)
        flat_ids = paired.reshape(-1)
        onehot = (flat_ids[:, None] == jnp.arange(EXPERTS, dtype=jnp.int32)[None, :]).astype(jnp.int32)
        earlier = jnp.cumsum(onehot, axis=0) - onehot
        slot_ids = jnp.sum(earlier * onehot, axis=1).reshape(TOK_DEV, 2)
        return (paired, slot_ids)

    def one_replica(replica_key):
        key_full, key_blocks = jax.random.split(replica_key)
        full_id = jax.random.randint(key_full, (), 0, EXPERTS)
        block_keys = jax.random.split(key_blocks, block_count)
        paired, slot_ids = jax.vmap(one_block, in_axes=(0, None))(block_keys, full_id)
        return (paired.reshape(LENGTH, 2), slot_ids.reshape(LENGTH, 2))
    return jax.vmap(one_replica)(jax.random.split(key, REPS))


def draw_experts(key, part):
    paired, slot_ids = routing_tables(jax.random.fold_in(key, 17))
    return paired


def draw_expert_slots(key, part):
    paired, slot_ids = routing_tables(jax.random.fold_in(key, 17))
    return slot_ids


def levels(key, shape, cuts, smallest, high):
    gain = 1.0
    for axis_at, shards_of in cuts:
        heights = jax.random.uniform(jax.random.fold_in(jax.random.fold_in(key, 6), axis_at), (shards_of,), jnp.float32, smallest / len(cuts), high / len(cuts))
        gain = gain * jnp.repeat(jnp.exp(heights), shape[axis_at] // shards_of).reshape((-1,) + (1,) * (len(shape) - 1 - axis_at))
    return gain


def normal_values(own_key, shape, width, reach, cuts=(), kind=jnp.bfloat16):
    loudness = levels(own_key, shape, cuts, -0.22, 0.18) if cuts else 1.0
    values = jax.random.normal(own_key, shape, jnp.float32) * width * loudness
    return jnp.minimum(jnp.maximum(values, -reach), reach).astype(kind)


def setup_inputs(seed: int = 0) -> dict:
    keys = jax.random.split(jax.random.key(seed), 17)
    return {
        "sequence": normal_values(keys[0], (REPS, LENGTH, D), 1.0, 6.0, ((0, 2), (1, 16))),
        "norm1_gain": jnp.clip(1.0 + 0.18 * jax.random.normal(keys[1], (D,), jnp.float32), 0.1, 1.9),
        "w_in": normal_values(keys[2], (D, 3, D), D ** -0.5, 0.125, ((2, 8),)),
        "long_filter": normal_values(keys[3], (LENGTH, D), LENGTH ** -0.5, 0.125, ((0, 16), (1, 8)), jnp.float32),
        "filter_decay": jnp.clip(jnp.exp(math.log(150.0) - 5.7037825 * jax.random.uniform(keys[4], (D,), jnp.float32) ** levels(keys[4], (D,), ((0, 8),), -0.2, 0.2)), 0.5, 150.0),
        "conv_bias": normal_values(keys[5], (D,), 1.0, 4.0, ((0, 8),), jnp.float32),
        "w_out": normal_values(keys[6], (D, D), D ** -0.5, 0.125, ((0, 8),)),
        "norm2_gain": jnp.clip(1.0 + 0.18 * jax.random.normal(keys[7], (D,), jnp.float32), 0.1, 1.9),
        "router": normal_values(keys[8], (D, EXPERTS), (3.0 / D ** 0.5), 0.39648438),
        "w_gate": normal_values(keys[9], (EXPERTS, D, HIDDEN_SIZE), D ** -0.5, 0.125, ((0, 8), (2, 16))),
        "w_up": normal_values(keys[10], (EXPERTS, D, HIDDEN_SIZE), D ** -0.5, 0.125, ((0, 8), (2, 16))),
        "w_down": normal_values(keys[11], (EXPERTS, HIDDEN_SIZE, D), HIDDEN_SIZE ** -0.5, 0.09375, ((0, 8), (1, 16))),
        "experts": draw_experts(jax.random.fold_in(keys[16], 71), 0),
        "expert_slots": draw_expert_slots(jax.random.fold_in(keys[16], 71), 0),
        "splice_head": normal_values(keys[14], (HEAD_OUT, D), D ** -0.5, 0.125),
        "targets": jnp.clip(1.0 * jax.random.uniform(keys[15], (REPS, LENGTH, HEAD_OUT), jnp.float32) ** levels(keys[15], (REPS, LENGTH, HEAD_OUT), ((0, 2), (1, 128)), -0.2, 0.2), 0.0, 1.0),
    }


def stored(values):
    return lax.optimization_barrier(values.astype(jnp.bfloat16))

def rms_scale(token_rows, norm_gain):
    wide = token_rows.astype(jnp.float32)
    inverse = lax.rsqrt(lax.optimization_barrier(jnp.mean(wide * wide, axis=-1, keepdims=True)) + 1e-05)
    return (wide * inverse * norm_gain).astype(jnp.bfloat16)

def run_expert(expert_pack):
    gate_all, up_all, down_all, routed_rows = expert_pack
    accum = jnp.zeros((routed_rows.shape[0], D), jnp.float32)
    for part_index in range(N_CTX):
        lower = part_index * HID_DEV
        upper = lower + HID_DEV
        gate_val = jnp.dot(routed_rows, gate_all[:, lower:upper], preferred_element_type=jnp.float32)
        up_val = jnp.dot(routed_rows, up_all[:, lower:upper], preferred_element_type=jnp.float32)
        slice_hidden = (jax.nn.silu(gate_val) * up_val).astype(jnp.bfloat16)
        slice_part = stored(jnp.dot(slice_hidden, down_all[lower:upper, :], preferred_element_type=jnp.float32))
        accum = accum + slice_part.astype(jnp.float32)
    return accum.astype(jnp.bfloat16)

def reference(sequence, norm1_gain, w_in, long_filter, filter_decay, conv_bias, w_out, norm2_gain, router, w_gate, w_up, w_down, experts, expert_slots, splice_head, targets):
    positions = jnp.arange(LENGTH, dtype=jnp.int32).astype(jnp.float32)
    shaped = long_filter * jnp.exp(-filter_decay[None, :] * positions[:, None] / LENGTH)
    filter_spectrum = jnp.fft.rfft(shaped, n=2 * LENGTH, axis=0)
    block_ids = (jnp.arange(LENGTH, dtype=jnp.int32) // TOK_DEV)[:, None] * jnp.ones((1, 2), jnp.int32)
    in_weights = w_in.astype(jnp.float32)
    loss_scale = 1.0 / math.sqrt(REPS * LENGTH)
    block_count = LENGTH // TOK_DEV
    results = []
    grad_total = jnp.zeros((HEAD_OUT, D), jnp.float32)
    for replica in range(REPS):
        tokens_in = sequence[replica]
        normed = rms_scale(tokens_in, norm1_gain)
        projected = jnp.einsum('ti,igd->tgd', normed.astype(jnp.float32), in_weights)
        source = projected[:, 1] * projected[:, 0]
        convolved = jnp.fft.irfft(jnp.fft.rfft(source, n=2 * LENGTH, axis=0) * filter_spectrum, n=2 * LENGTH, axis=0)[:LENGTH]
        gated_rows = (projected[:, 2] * (convolved + conv_bias[None, :] * source)).astype(jnp.bfloat16)
        hidden_state = stored(tokens_in.astype(jnp.float32) + jnp.dot(gated_rows, w_out, preferred_element_type=jnp.float32))
        routed_in = rms_scale(hidden_state, norm2_gain)
        chances = jax.nn.sigmoid(jnp.dot(routed_in, router, preferred_element_type=jnp.float32))
        picked_ids = experts[replica]
        slot_ids = expert_slots[replica]
        chosen = jnp.take_along_axis(chances, picked_ids, axis=1)
        weights = chosen / lax.optimization_barrier(jnp.sum(chosen, axis=1, keepdims=True))
        buffer = jnp.zeros((EXPERTS, block_count, CAP, D), jnp.bfloat16)
        values = jnp.broadcast_to(routed_in[:, None, :], (LENGTH, 2, D))
        buffer = buffer.at[picked_ids, block_ids, slot_ids].set(values)
        expert_all = lax.map(run_expert, (w_gate, w_up, w_down, buffer.reshape(EXPERTS, block_count * CAP, D)))
        expert_all = expert_all.reshape(EXPERTS, block_count, CAP, D)
        picked = expert_all[picked_ids, block_ids, slot_ids].astype(jnp.float32)
        combined = weights[:, 0:1] * picked[:, 0] + weights[:, 1:2] * picked[:, 1]
        block_final = stored(hidden_state.astype(jnp.float32) + combined)
        usage_prob = jax.nn.sigmoid(jnp.dot(block_final, splice_head.T, preferred_element_type=jnp.float32))
        usage_grad = ((usage_prob - targets[replica]) * loss_scale).astype(jnp.bfloat16)
        grad_total = grad_total + jnp.dot(usage_grad.T, block_final, preferred_element_type=jnp.float32)
        results.append(block_final)
    return (jnp.stack(results, axis=0), grad_total)
```

```python
import math

import jax
import jax.numpy as jnp
from jax import lax
from jax.sharding import PartitionSpec as P

TWO_PI = 2.0 * math.pi


def stored(values):
    return lax.optimization_barrier(values.astype(jnp.bfloat16))


def rms_scale(token_rows, norm_gain):
    wide = token_rows.astype(jnp.float32)
    inverse = lax.rsqrt(jnp.mean(wide * wide, axis=-1, keepdims=True) + 1e-05)
    return (wide * inverse * norm_gain).astype(jnp.bfloat16)


def phase_table(first_ids, second_ids, modulus):
    angle = (
        TWO_PI * (first_ids[:, None] * second_ids[None, :] % modulus).astype(jnp.float32) / modulus
    )
    return (jnp.cos(angle), jnp.sin(angle))


def spectra_move(blocks):
    return lax.all_to_all(blocks, "ctx", split_axis=0, concat_axis=1, tiled=True)


def a2a_reduce(values, axes):
    count = lax.axis_size(axes)
    pieces = lax.all_to_all(values.reshape(count, -1), axes, 0, 0, tiled=True)
    return jnp.sum(pieces, axis=0)


def a2a_allreduce(values, axes):
    count = lax.axis_size(axes)
    if values.size % count:
        return lax.psum(values, axes)
    mine = a2a_reduce(values, axes)
    spread = jnp.broadcast_to(mine[None], (count,) + mine.shape)
    return lax.all_to_all(spread, axes, 0, 0, tiled=True).reshape(values.shape)


def token_move(blocks):
    return lax.all_to_all(blocks, ("ctx", "exp"), split_axis=0, concat_axis=0, tiled=True)


def causal_convolve(source, shaped):
    highest = lax.Precision.HIGHEST
    ctx_count = lax.axis_size("ctx")
    ctx_pos = lax.axis_index("ctx")
    local_rows, channels = source.shape
    sub_rows = local_rows // ctx_count
    halves = 2 * ctx_count
    points = halves * local_rows
    block_ids = jnp.arange(ctx_count, dtype=jnp.int32)
    freq_ids = jnp.arange(halves, dtype=jnp.int32)
    cos_outer, sin_outer = phase_table(block_ids, freq_ids, halves)
    gathered = spectra_move(jnp.stack([source, shaped], axis=1)).reshape(
        sub_rows, ctx_count, 2, channels
    )
    real_a = jnp.einsum("qcmx,ck->kqmx", gathered, cos_outer, precision=highest)
    imag_a = -jnp.einsum("qcmx,ck->kqmx", gathered, sin_outer, precision=highest)
    positions = ctx_pos * sub_rows + jnp.arange(sub_rows, dtype=jnp.int32)
    cos_twist, sin_twist = phase_table(freq_ids, positions, points)
    cos_twist = cos_twist[:, :, None, None]
    sin_twist = sin_twist[:, :, None, None]
    real_b = real_a * cos_twist + imag_a * sin_twist
    imag_b = imag_a * cos_twist - real_a * sin_twist
    spread = spectra_move(jnp.concatenate([real_b, imag_b], axis=2))
    row_ids = jnp.arange(local_rows, dtype=jnp.int32)
    cos_inner, sin_inner = phase_table(row_ids, row_ids, local_rows)
    cos_part = jnp.einsum("kpzx,pq->kqzx", spread, cos_inner, precision=highest)
    sin_part = jnp.einsum("kpzx,pq->kqzx", spread, sin_inner, precision=highest)
    real_f = cos_part[:, :, 0:2] + sin_part[:, :, 2:4]
    imag_f = cos_part[:, :, 2:4] - sin_part[:, :, 0:2]
    real_z = real_f[:, :, 0] * real_f[:, :, 1] - imag_f[:, :, 0] * imag_f[:, :, 1]
    imag_z = real_f[:, :, 0] * imag_f[:, :, 1] + imag_f[:, :, 0] * real_f[:, :, 1]
    product = jnp.stack([real_z, imag_z], axis=2)
    cos_back = jnp.einsum("kqrx,qp->pkrx", product, cos_inner, precision=highest)
    sin_back = jnp.einsum("kqrx,qp->pkrx", product, sin_inner, precision=highest)
    real_w = cos_back[:, :, 0] - sin_back[:, :, 1]
    imag_w = cos_back[:, :, 1] + sin_back[:, :, 0]
    returned = spectra_move(jnp.stack([real_w, imag_w], axis=2))
    cos_again, sin_again = phase_table(positions, freq_ids, points)
    cos_again = cos_again[:, :, None]
    sin_again = sin_again[:, :, None]
    real_v = returned[:, :, 0] * cos_again - returned[:, :, 1] * sin_again
    imag_v = returned[:, :, 1] * cos_again + returned[:, :, 0] * sin_again
    blocks_out = (
        jnp.einsum("qkx,ck->cqx", real_v, cos_outer, precision=highest)
        - jnp.einsum("qkx,ck->cqx", imag_v, sin_outer, precision=highest)
    ) / points
    return spectra_move(blocks_out)[0]


def shards(
    sequence,
    norm1_gain,
    w_in,
    long_filter,
    filter_decay,
    conv_bias,
    w_out,
    norm2_gain,
    router,
    w_gate,
    w_up,
    w_down,
    experts,
    expert_slots,
    splice_head,
    targets,
):
    exp_count = lax.axis_size("exp")
    exp_pos = lax.axis_index("exp")
    ctx_count = lax.axis_size("ctx")
    ctx_pos = lax.axis_index("ctx")
    local_x = sequence[0]
    local_rows, model_width = local_x.shape
    own_rows = local_rows // exp_count
    length = local_rows * ctx_count
    normed = rms_scale(local_x, norm1_gain)
    projected = jnp.einsum("ti,igd->tgd", normed, w_in, preferred_element_type=jnp.float32)
    source = projected[:, 1] * projected[:, 0]
    positions = (ctx_pos * local_rows + jnp.arange(local_rows, dtype=jnp.int32)).astype(jnp.float32)
    shaped = long_filter * jnp.exp(-filter_decay[None, :] * positions[:, None] / length)
    convolved = causal_convolve(source, shaped)
    gated_rows = (projected[:, 2] * (convolved + conv_bias[None, :] * source)).astype(jnp.bfloat16)
    mixed_full = jnp.dot(gated_rows, w_out, preferred_element_type=jnp.float32)
    mixed_sum = a2a_reduce(mixed_full.reshape(exp_count, own_rows * model_width), "exp").reshape(
        own_rows, model_width
    )
    residual_rows = lax.dynamic_slice_in_dim(local_x, exp_pos * own_rows, own_rows, 0)
    hidden_state = stored(residual_rows.astype(jnp.float32) + mixed_sum)
    routed_in = rms_scale(hidden_state, norm2_gain)
    chances = jax.nn.sigmoid(jnp.dot(routed_in, router, preferred_element_type=jnp.float32))
    picked_ids = experts[0]
    slot_ids = expert_slots[0]
    chosen = jnp.take_along_axis(chances, picked_ids, axis=1)
    weights = chosen / jnp.sum(chosen, axis=1, keepdims=True)
    n_experts = router.shape[1]
    capacity = 4 * own_rows // exp_count
    slot_rows = picked_ids * capacity + slot_ids
    buffer_ids = jnp.arange(n_experts * capacity, dtype=jnp.int32)[:, None]
    selector = (
        (slot_rows[None, :, 0] == buffer_ids) | (slot_rows[None, :, 1] == buffer_ids)
    ).astype(jnp.bfloat16)
    outgoing = jnp.dot(selector, routed_in, preferred_element_type=jnp.float32).astype(jnp.bfloat16)
    outgoing = outgoing.reshape(n_experts, capacity, model_width)
    gate_local = w_gate[0]
    up_local = w_up[0]
    down_local = w_down[0]
    copies = jnp.broadcast_to(outgoing[None], (ctx_count, n_experts, capacity, model_width))
    arrived = token_move(copies.reshape(ctx_count * n_experts, capacity, model_width))
    token_rows = arrived.reshape(-1, model_width)
    gate_val = jnp.dot(token_rows, gate_local, preferred_element_type=jnp.float32)
    up_val = jnp.dot(token_rows, up_local, preferred_element_type=jnp.float32)
    slice_hidden = (jax.nn.silu(gate_val) * up_val).astype(jnp.bfloat16)
    slice_part = (
        jnp.dot(slice_hidden, down_local, preferred_element_type=jnp.float32)
        .astype(jnp.bfloat16)
        .reshape(ctx_count * n_experts, capacity, model_width)
    )
    came_back = token_move(slice_part)
    summed = jnp.sum(
        came_back.reshape(ctx_count, n_experts, capacity, model_width).astype(jnp.float32), axis=0
    )
    expert_out = stored(summed)
    flat_out = expert_out.reshape(n_experts * capacity, model_width)
    first_rows = jnp.take(flat_out, slot_rows[:, 0], axis=0).astype(jnp.float32)
    second_rows = jnp.take(flat_out, slot_rows[:, 1], axis=0).astype(jnp.float32)
    combined = weights[:, 0:1] * first_rows + weights[:, 1:2] * second_rows
    block_final = stored(hidden_state.astype(jnp.float32) + combined)
    usage_prob = jax.nn.sigmoid(
        jnp.einsum("td,od->to", block_final, splice_head, preferred_element_type=jnp.float32)
    )
    all_tokens = lax.axis_size("rep") * ctx_count * exp_count * own_rows
    loss_scale = 1.0 / math.sqrt(all_tokens)
    usage_grad = ((usage_prob - targets[0]) * loss_scale).astype(jnp.bfloat16)
    local_grad = jnp.einsum(
        "to,td->od", usage_grad, block_final, preferred_element_type=jnp.float32
    )
    head_total = a2a_allreduce(local_grad, ("ctx", "exp", "rep"))
    return (block_final[None], head_total)


def solution(mesh):
    in_specs = (
        P("rep", "ctx", None),
        P(),
        P(None, None, "exp"),
        P("ctx", "exp"),
        P("exp"),
        P("exp"),
        P("exp", None),
        P(),
        P(),
        P("exp", None, "ctx"),
        P("exp", None, "ctx"),
        P("exp", "ctx", None),
        P("rep", ("ctx", "exp"), None),
        P("rep", ("ctx", "exp"), None),
        P(),
        P("rep", ("ctx", "exp"), None),
    )
    out_specs = (P("rep", ("ctx", "exp"), None), P())
    return jax.shard_map(shards, mesh=mesh, in_specs=in_specs, out_specs=out_specs, check_vma=False)
```

```python
import math

import jax
import jax.numpy as jnp
from jax import lax
from jax.sharding import PartitionSpec as P

TWO_PI = 2.0 * math.pi


def stored(values):
    return lax.optimization_barrier(values.astype(jnp.bfloat16))


def rms_scale(token_rows, norm_gain):
    wide = token_rows.astype(jnp.float32)
    inverse = lax.rsqrt(jnp.mean(wide * wide, axis=-1, keepdims=True) + 1e-05)
    return (wide * inverse * norm_gain).astype(jnp.bfloat16)


def phase_table(first_ids, second_ids, modulus):
    angle = (
        TWO_PI * (first_ids[:, None] * second_ids[None, :] % modulus).astype(jnp.float32) / modulus
    )
    return (jnp.cos(angle), jnp.sin(angle))


def spectra_move(blocks):
    return lax.all_to_all(blocks, "ctx", split_axis=0, concat_axis=1, tiled=True)


def a2a_reduce(values, axes):
    count = lax.axis_size(axes)
    pieces = lax.all_to_all(values.reshape(count, -1), axes, 0, 0, tiled=True)
    return jnp.sum(pieces, axis=0)


def a2a_allreduce(values, axes):
    count = lax.axis_size(axes)
    if values.size % count:
        return lax.psum(values, axes)
    mine = a2a_reduce(values, axes)
    spread = jnp.broadcast_to(mine[None], (count,) + mine.shape)
    return lax.all_to_all(spread, axes, 0, 0, tiled=True).reshape(values.shape)


def token_move(blocks):
    return lax.all_to_all(blocks, ("ctx", "exp"), split_axis=0, concat_axis=0, tiled=True)


def causal_convolve(source, shaped):
    ctx_count = lax.axis_size("ctx")
    local_rows, channels = source.shape
    length = local_rows * ctx_count
    both = jnp.stack([source, shaped], axis=1)
    whole = lax.all_to_all(both, "ctx", split_axis=2, concat_axis=0, tiled=True)
    spectra = jnp.fft.rfft(whole, n=2 * length, axis=0)
    convolved = jnp.fft.irfft(spectra[:, 0] * spectra[:, 1], n=2 * length, axis=0)[:length]
    return lax.all_to_all(convolved, "ctx", split_axis=0, concat_axis=1, tiled=True)


def shards(
    sequence,
    norm1_gain,
    w_in,
    long_filter,
    filter_decay,
    conv_bias,
    w_out,
    norm2_gain,
    router,
    w_gate,
    w_up,
    w_down,
    experts,
    expert_slots,
    splice_head,
    targets,
):
    exp_count = lax.axis_size("exp")
    exp_pos = lax.axis_index("exp")
    ctx_count = lax.axis_size("ctx")
    ctx_pos = lax.axis_index("ctx")
    local_x = sequence[0]
    local_rows, model_width = local_x.shape
    own_rows = local_rows // exp_count
    length = local_rows * ctx_count
    normed = rms_scale(local_x, norm1_gain)
    projected = jnp.einsum("ti,igd->tgd", normed, w_in, preferred_element_type=jnp.float32)
    source = projected[:, 1] * projected[:, 0]
    positions = (ctx_pos * local_rows + jnp.arange(local_rows, dtype=jnp.int32)).astype(jnp.float32)
    shaped = long_filter * jnp.exp(-filter_decay[None, :] * positions[:, None] / length)
    convolved = causal_convolve(source, shaped)
    gated_rows = (projected[:, 2] * (convolved + conv_bias[None, :] * source)).astype(jnp.bfloat16)
    mixed_full = jnp.dot(gated_rows, w_out, preferred_element_type=jnp.float32)
    mixed_sum = a2a_reduce(mixed_full.reshape(exp_count, own_rows * model_width), "exp").reshape(
        own_rows, model_width
    )
    residual_rows = lax.dynamic_slice_in_dim(local_x, exp_pos * own_rows, own_rows, 0)
    hidden_state = stored(residual_rows.astype(jnp.float32) + mixed_sum)
    routed_in = rms_scale(hidden_state, norm2_gain)
    chances = jax.nn.sigmoid(jnp.dot(routed_in, router, preferred_element_type=jnp.float32))
    picked_ids = experts[0]
    slot_ids = expert_slots[0]
    chosen = jnp.take_along_axis(chances, picked_ids, axis=1)
    weights = chosen / jnp.sum(chosen, axis=1, keepdims=True)
    n_experts = router.shape[1]
    capacity = 4 * own_rows // exp_count
    slot_rows = picked_ids * capacity + slot_ids
    buffer_ids = jnp.arange(n_experts * capacity, dtype=jnp.int32)[:, None]
    selector = (
        (slot_rows[None, :, 0] == buffer_ids) | (slot_rows[None, :, 1] == buffer_ids)
    ).astype(jnp.bfloat16)
    outgoing = jnp.dot(selector, routed_in, preferred_element_type=jnp.float32).astype(jnp.bfloat16)
    outgoing = outgoing.reshape(n_experts, capacity, model_width)
    gate_local = w_gate[0]
    up_local = w_up[0]
    down_local = w_down[0]
    copies = jnp.broadcast_to(outgoing[None], (ctx_count, n_experts, capacity, model_width))
    arrived = token_move(copies.reshape(ctx_count * n_experts, capacity, model_width))
    token_rows = arrived.reshape(-1, model_width)
    gate_val = jnp.dot(token_rows, gate_local, preferred_element_type=jnp.float32)
    up_val = jnp.dot(token_rows, up_local, preferred_element_type=jnp.float32)
    slice_hidden = (jax.nn.silu(gate_val) * up_val).astype(jnp.bfloat16)
    slice_part = (
        jnp.dot(slice_hidden, down_local, preferred_element_type=jnp.float32)
        .astype(jnp.bfloat16)
        .reshape(ctx_count * n_experts, capacity, model_width)
    )
    came_back = token_move(slice_part)
    summed = jnp.sum(
        came_back.reshape(ctx_count, n_experts, capacity, model_width).astype(jnp.float32), axis=0
    )
    expert_out = stored(summed)
    flat_out = expert_out.reshape(n_experts * capacity, model_width)
    first_rows = jnp.take(flat_out, slot_rows[:, 0], axis=0).astype(jnp.float32)
    second_rows = jnp.take(flat_out, slot_rows[:, 1], axis=0).astype(jnp.float32)
    combined = weights[:, 0:1] * first_rows + weights[:, 1:2] * second_rows
    block_final = stored(hidden_state.astype(jnp.float32) + combined)
    usage_prob = jax.nn.sigmoid(
        jnp.einsum("td,od->to", block_final, splice_head, preferred_element_type=jnp.float32)
    )
    all_tokens = lax.axis_size("rep") * ctx_count * exp_count * own_rows
    loss_scale = 1.0 / math.sqrt(all_tokens)
    usage_grad = ((usage_prob - targets[0]) * loss_scale).astype(jnp.bfloat16)
    local_grad = jnp.einsum(
        "to,td->od", usage_grad, block_final, preferred_element_type=jnp.float32
    )
    head_total = a2a_allreduce(local_grad, ("ctx", "exp", "rep"))
    return (block_final[None], head_total)


def solution(mesh):
    in_specs = (
        P("rep", "ctx", None),
        P(),
        P(None, None, "exp"),
        P("ctx", "exp"),
        P("exp"),
        P("exp"),
        P("exp", None),
        P(),
        P(),
        P("exp", None, "ctx"),
        P("exp", None, "ctx"),
        P("exp", "ctx", None),
        P("rep", ("ctx", "exp"), None),
        P("rep", ("ctx", "exp"), None),
        P(),
        P("rep", ("ctx", "exp"), None),
    )
    out_specs = (P("rep", ("ctx", "exp"), None), P())
    return jax.shard_map(shards, mesh=mesh, in_specs=in_specs, out_specs=out_specs, check_vma=False)
```

```python
import math

import jax
import jax.numpy as jnp
from jax import lax
from jax.sharding import PartitionSpec as P

TWO_PI = 2.0 * math.pi


def stored(values):
    return lax.optimization_barrier(values.astype(jnp.bfloat16))


def rms_scale(token_rows, norm_gain):
    wide = token_rows.astype(jnp.float32)
    inverse = lax.rsqrt(jnp.mean(wide * wide, axis=-1, keepdims=True) + 1e-05)
    return (wide * inverse * norm_gain).astype(jnp.bfloat16)


def phase_table(first_ids, second_ids, modulus):
    angle = (
        TWO_PI * (first_ids[:, None] * second_ids[None, :] % modulus).astype(jnp.float32) / modulus
    )
    return (jnp.cos(angle), jnp.sin(angle))


def spectra_move(blocks):
    return lax.all_to_all(blocks, "ctx", split_axis=0, concat_axis=1, tiled=True)


def a2a_reduce(values, axes, wire=None):
    count = lax.axis_size(axes)
    sent = values.reshape(count, -1)
    if wire is not None:
        sent = sent.astype(wire)
    pieces = lax.all_to_all(sent, axes, 0, 0, tiled=True)
    return jnp.sum(pieces.astype(jnp.float32), axis=0)


def a2a_allreduce(values, axes, wire=None):
    count = lax.axis_size(axes)
    if values.size % count:
        return lax.psum(values, axes)
    mine = a2a_reduce(values, axes, wire)
    if wire is not None:
        mine = mine.astype(wire)
    spread = jnp.broadcast_to(mine[None], (count,) + mine.shape)
    gathered = lax.all_to_all(spread, axes, 0, 0, tiled=True)
    return gathered.astype(jnp.float32).reshape(values.shape)


def token_move(blocks):
    return lax.all_to_all(blocks, ("ctx", "exp"), split_axis=0, concat_axis=0, tiled=True)


def causal_convolve(source, shaped):
    highest = lax.Precision.HIGHEST
    ctx_count = lax.axis_size("ctx")
    ctx_pos = lax.axis_index("ctx")
    local_rows, channels = source.shape
    sub_rows = local_rows // ctx_count
    halves = 2 * ctx_count
    points = halves * local_rows
    block_ids = jnp.arange(ctx_count, dtype=jnp.int32)
    freq_ids = jnp.arange(halves, dtype=jnp.int32)
    cos_outer, sin_outer = phase_table(block_ids, freq_ids, halves)
    gathered = spectra_move(jnp.stack([source, shaped], axis=1)).reshape(
        sub_rows, ctx_count, 2, channels
    )
    real_a = jnp.einsum("qcmx,ck->kqmx", gathered, cos_outer, precision=highest)
    imag_a = -jnp.einsum("qcmx,ck->kqmx", gathered, sin_outer, precision=highest)
    positions = ctx_pos * sub_rows + jnp.arange(sub_rows, dtype=jnp.int32)
    cos_twist, sin_twist = phase_table(freq_ids, positions, points)
    cos_twist = cos_twist[:, :, None, None]
    sin_twist = sin_twist[:, :, None, None]
    real_b = real_a * cos_twist + imag_a * sin_twist
    imag_b = imag_a * cos_twist - real_a * sin_twist
    spread = spectra_move(jnp.concatenate([real_b, imag_b], axis=2))
    row_ids = jnp.arange(local_rows, dtype=jnp.int32)
    cos_inner, sin_inner = phase_table(row_ids, row_ids, local_rows)
    cos_part = jnp.einsum("kpzx,pq->kqzx", spread, cos_inner, precision=highest)
    sin_part = jnp.einsum("kpzx,pq->kqzx", spread, sin_inner, precision=highest)
    real_f = cos_part[:, :, 0:2] + sin_part[:, :, 2:4]
    imag_f = cos_part[:, :, 2:4] - sin_part[:, :, 0:2]
    real_z = real_f[:, :, 0] * real_f[:, :, 1] - imag_f[:, :, 0] * imag_f[:, :, 1]
    imag_z = real_f[:, :, 0] * imag_f[:, :, 1] + imag_f[:, :, 0] * real_f[:, :, 1]
    product = jnp.stack([real_z, imag_z], axis=2)
    cos_back = jnp.einsum("kqrx,qp->pkrx", product, cos_inner, precision=highest)
    sin_back = jnp.einsum("kqrx,qp->pkrx", product, sin_inner, precision=highest)
    real_w = cos_back[:, :, 0] - sin_back[:, :, 1]
    imag_w = cos_back[:, :, 1] + sin_back[:, :, 0]
    returned = spectra_move(jnp.stack([real_w, imag_w], axis=2))
    cos_again, sin_again = phase_table(positions, freq_ids, points)
    cos_again = cos_again[:, :, None]
    sin_again = sin_again[:, :, None]
    real_v = returned[:, :, 0] * cos_again - returned[:, :, 1] * sin_again
    imag_v = returned[:, :, 1] * cos_again + returned[:, :, 0] * sin_again
    blocks_out = (
        jnp.einsum("qkx,ck->cqx", real_v, cos_outer, precision=highest)
        - jnp.einsum("qkx,ck->cqx", imag_v, sin_outer, precision=highest)
    ) / points
    return spectra_move(blocks_out)[0]


def shards(
    sequence,
    norm1_gain,
    w_in,
    long_filter,
    filter_decay,
    conv_bias,
    w_out,
    norm2_gain,
    router,
    w_gate,
    w_up,
    w_down,
    experts,
    expert_slots,
    splice_head,
    targets,
):
    exp_count = lax.axis_size("exp")
    exp_pos = lax.axis_index("exp")
    ctx_count = lax.axis_size("ctx")
    ctx_pos = lax.axis_index("ctx")
    local_x = sequence[0]
    local_rows, model_width = local_x.shape
    own_rows = local_rows // exp_count
    length = local_rows * ctx_count
    normed = rms_scale(local_x, norm1_gain)
    projected = jnp.einsum("ti,igd->tgd", normed, w_in, preferred_element_type=jnp.float32)
    source = projected[:, 1] * projected[:, 0]
    positions = (ctx_pos * local_rows + jnp.arange(local_rows, dtype=jnp.int32)).astype(jnp.float32)
    shaped = long_filter * jnp.exp(-filter_decay[None, :] * positions[:, None] / length)
    convolved = causal_convolve(source, shaped)
    gated_rows = (projected[:, 2] * (convolved + conv_bias[None, :] * source)).astype(jnp.bfloat16)
    mixed_full = jnp.dot(gated_rows, w_out, preferred_element_type=jnp.float32)
    mixed_sum = a2a_reduce(mixed_full.reshape(exp_count, own_rows * model_width), "exp").reshape(
        own_rows, model_width
    )
    residual_rows = lax.dynamic_slice_in_dim(local_x, exp_pos * own_rows, own_rows, 0)
    hidden_state = stored(residual_rows.astype(jnp.float32) + mixed_sum)
    routed_in = rms_scale(hidden_state, norm2_gain)
    chances = jax.nn.sigmoid(jnp.dot(routed_in, router, preferred_element_type=jnp.float32))
    picked_ids = experts[0]
    slot_ids = expert_slots[0]
    chosen = jnp.take_along_axis(chances, picked_ids, axis=1)
    weights = chosen / jnp.sum(chosen, axis=1, keepdims=True)
    n_experts = router.shape[1]
    capacity = 4 * own_rows // exp_count
    slot_rows = picked_ids * capacity + slot_ids
    buffer_ids = jnp.arange(n_experts * capacity, dtype=jnp.int32)[:, None]
    selector = (
        (slot_rows[None, :, 0] == buffer_ids) | (slot_rows[None, :, 1] == buffer_ids)
    ).astype(jnp.bfloat16)
    outgoing = jnp.dot(selector, routed_in, preferred_element_type=jnp.float32).astype(jnp.bfloat16)
    outgoing = outgoing.reshape(n_experts, capacity, model_width)
    gate_local = w_gate[0]
    up_local = w_up[0]
    down_local = w_down[0]
    copies = jnp.broadcast_to(outgoing[None], (ctx_count, n_experts, capacity, model_width))
    arrived = token_move(copies.reshape(ctx_count * n_experts, capacity, model_width))
    token_rows = arrived.reshape(-1, model_width)
    gate_val = jnp.dot(token_rows, gate_local, preferred_element_type=jnp.float32)
    up_val = jnp.dot(token_rows, up_local, preferred_element_type=jnp.float32)
    slice_hidden = (jax.nn.silu(gate_val) * up_val).astype(jnp.bfloat16)
    slice_part = (
        jnp.dot(slice_hidden, down_local, preferred_element_type=jnp.float32)
        .astype(jnp.bfloat16)
        .reshape(ctx_count * n_experts, capacity, model_width)
    )
    came_back = token_move(slice_part)
    summed = jnp.sum(
        came_back.reshape(ctx_count, n_experts, capacity, model_width).astype(jnp.float32), axis=0
    )
    expert_out = stored(summed)
    flat_out = expert_out.reshape(n_experts * capacity, model_width)
    first_rows = jnp.take(flat_out, slot_rows[:, 0], axis=0).astype(jnp.float32)
    second_rows = jnp.take(flat_out, slot_rows[:, 1], axis=0).astype(jnp.float32)
    combined = weights[:, 0:1] * first_rows + weights[:, 1:2] * second_rows
    block_final = stored(hidden_state.astype(jnp.float32) + combined)
    usage_prob = jax.nn.sigmoid(
        jnp.einsum("td,od->to", block_final, splice_head, preferred_element_type=jnp.float32)
    )
    all_tokens = lax.axis_size("rep") * ctx_count * exp_count * own_rows
    loss_scale = 1.0 / math.sqrt(all_tokens)
    usage_grad = ((usage_prob - targets[0]) * loss_scale).astype(jnp.bfloat16)
    local_grad = jnp.einsum(
        "to,td->od", usage_grad, block_final, preferred_element_type=jnp.float32
    )
    head_total = a2a_allreduce(local_grad, ("ctx", "exp", "rep"), jnp.bfloat16)
    return (block_final[None], head_total)


def solution(mesh):
    in_specs = (
        P("rep", "ctx", None),
        P(),
        P(None, None, "exp"),
        P("ctx", "exp"),
        P("exp"),
        P("exp"),
        P("exp", None),
        P(),
        P(),
        P("exp", None, "ctx"),
        P("exp", None, "ctx"),
        P("exp", "ctx", None),
        P("rep", ("ctx", "exp"), None),
        P("rep", ("ctx", "exp"), None),
        P(),
        P("rep", ("ctx", "exp"), None),
    )
    out_specs = (P("rep", ("ctx", "exp"), None), P())
    return jax.shard_map(shards, mesh=mesh, in_specs=in_specs, out_specs=out_specs, check_vma=False)
```

```python
import math

import jax
import jax.numpy as jnp
from jax import lax
from jax.sharding import PartitionSpec as P

TWO_PI = 2.0 * math.pi


def stored(values):
    return lax.optimization_barrier(values.astype(jnp.bfloat16))


def rms_scale(token_rows, norm_gain):
    wide = token_rows.astype(jnp.float32)
    inverse = lax.rsqrt(jnp.mean(wide * wide, axis=-1, keepdims=True) + 1e-05)
    return (wide * inverse * norm_gain).astype(jnp.bfloat16)


def phase_table(first_ids, second_ids, modulus):
    angle = (
        TWO_PI * (first_ids[:, None] * second_ids[None, :] % modulus).astype(jnp.float32) / modulus
    )
    return (jnp.cos(angle), jnp.sin(angle))


def spectra_move(blocks):
    return lax.all_to_all(blocks, "ctx", split_axis=0, concat_axis=1, tiled=True)


def a2a_reduce(values, axes, wire=None):
    count = lax.axis_size(axes)
    sent = values.reshape((count, -1) + values.shape[1:])
    if wire is not None:
        sent = sent.astype(wire)
    pieces = lax.all_to_all(sent, axes, 0, 0, tiled=True)
    return jnp.sum(pieces.astype(jnp.float32), axis=0)


def a2a_allreduce(values, axes, wire=None):
    count = lax.axis_size(axes)
    if values.shape[0] % count:
        return lax.psum(values, axes)
    mine = a2a_reduce(values, axes, wire)
    if wire is not None:
        mine = mine.astype(wire)
    spread = jnp.broadcast_to(mine[None], (count,) + mine.shape)
    gathered = lax.all_to_all(spread, axes, 0, 0, tiled=True)
    return gathered.astype(jnp.float32).reshape(values.shape)


def token_move(blocks):
    return lax.all_to_all(blocks, ("ctx", "exp"), split_axis=0, concat_axis=0, tiled=True)


def causal_convolve(source, shaped):
    highest = lax.Precision.HIGHEST
    ctx_count = lax.axis_size("ctx")
    ctx_pos = lax.axis_index("ctx")
    local_rows, channels = source.shape
    sub_rows = local_rows // ctx_count
    halves = 2 * ctx_count
    points = halves * local_rows
    block_ids = jnp.arange(ctx_count, dtype=jnp.int32)
    freq_ids = jnp.arange(halves, dtype=jnp.int32)
    cos_outer, sin_outer = phase_table(block_ids, freq_ids, halves)
    gathered = spectra_move(jnp.stack([source, shaped], axis=1)).reshape(
        sub_rows, ctx_count, 2, channels
    )
    real_a = jnp.einsum("qcmx,ck->kqmx", gathered, cos_outer, precision=highest)
    imag_a = -jnp.einsum("qcmx,ck->kqmx", gathered, sin_outer, precision=highest)
    positions = ctx_pos * sub_rows + jnp.arange(sub_rows, dtype=jnp.int32)
    cos_twist, sin_twist = phase_table(freq_ids, positions, points)
    cos_twist = cos_twist[:, :, None, None]
    sin_twist = sin_twist[:, :, None, None]
    real_b = real_a * cos_twist + imag_a * sin_twist
    imag_b = imag_a * cos_twist - real_a * sin_twist
    spread = spectra_move(jnp.concatenate([real_b, imag_b], axis=2))
    row_ids = jnp.arange(local_rows, dtype=jnp.int32)
    cos_inner, sin_inner = phase_table(row_ids, row_ids, local_rows)
    cos_part = jnp.einsum("kpzx,pq->kqzx", spread, cos_inner, precision=highest)
    sin_part = jnp.einsum("kpzx,pq->kqzx", spread, sin_inner, precision=highest)
    real_f = cos_part[:, :, 0:2] + sin_part[:, :, 2:4]
    imag_f = cos_part[:, :, 2:4] - sin_part[:, :, 0:2]
    real_z = real_f[:, :, 0] * real_f[:, :, 1] - imag_f[:, :, 0] * imag_f[:, :, 1]
    imag_z = real_f[:, :, 0] * imag_f[:, :, 1] + imag_f[:, :, 0] * real_f[:, :, 1]
    product = jnp.stack([real_z, imag_z], axis=2)
    cos_back = jnp.einsum("kqrx,qp->pkrx", product, cos_inner, precision=highest)
    sin_back = jnp.einsum("kqrx,qp->pkrx", product, sin_inner, precision=highest)
    real_w = cos_back[:, :, 0] - sin_back[:, :, 1]
    imag_w = cos_back[:, :, 1] + sin_back[:, :, 0]
    returned = spectra_move(jnp.stack([real_w, imag_w], axis=2))
    cos_again, sin_again = phase_table(positions, freq_ids, points)
    cos_again = cos_again[:, :, None]
    sin_again = sin_again[:, :, None]
    real_v = returned[:, :, 0] * cos_again - returned[:, :, 1] * sin_again
    imag_v = returned[:, :, 1] * cos_again + returned[:, :, 0] * sin_again
    blocks_out = (
        jnp.einsum("qkx,ck->cqx", real_v, cos_outer, precision=highest)
        - jnp.einsum("qkx,ck->cqx", imag_v, sin_outer, precision=highest)
    ) / points
    return spectra_move(blocks_out)[0]


def shards(
    sequence,
    norm1_gain,
    w_in,
    long_filter,
    filter_decay,
    conv_bias,
    w_out,
    norm2_gain,
    router,
    w_gate,
    w_up,
    w_down,
    experts,
    expert_slots,
    splice_head,
    targets,
):
    exp_count = lax.axis_size("exp")
    exp_pos = lax.axis_index("exp")
    ctx_count = lax.axis_size("ctx")
    ctx_pos = lax.axis_index("ctx")
    local_x = sequence[0]
    local_rows, model_width = local_x.shape
    own_rows = local_rows // exp_count
    length = local_rows * ctx_count
    normed = rms_scale(local_x, norm1_gain)
    projected = jnp.einsum("ti,igd->tgd", normed, w_in, preferred_element_type=jnp.float32)
    source = projected[:, 1] * projected[:, 0]
    positions = (ctx_pos * local_rows + jnp.arange(local_rows, dtype=jnp.int32)).astype(jnp.float32)
    shaped = long_filter * jnp.exp(-filter_decay[None, :] * positions[:, None] / length)
    convolved = causal_convolve(source, shaped)
    gated_rows = (projected[:, 2] * (convolved + conv_bias[None, :] * source)).astype(jnp.bfloat16)
    mixed_full = jnp.dot(gated_rows, w_out, preferred_element_type=jnp.float32)
    mixed_sum = a2a_reduce(mixed_full, "exp")
    residual_rows = lax.dynamic_slice_in_dim(local_x, exp_pos * own_rows, own_rows, 0)
    hidden_state = stored(residual_rows.astype(jnp.float32) + mixed_sum)
    routed_in = rms_scale(hidden_state, norm2_gain)
    chances = jax.nn.sigmoid(jnp.dot(routed_in, router, preferred_element_type=jnp.float32))
    picked_ids = experts[0]
    slot_ids = expert_slots[0]
    chosen = jnp.take_along_axis(chances, picked_ids, axis=1)
    weights = chosen / jnp.sum(chosen, axis=1, keepdims=True)
    n_experts = router.shape[1]
    capacity = 4 * own_rows // exp_count
    slot_rows = picked_ids * capacity + slot_ids
    buffer_ids = jnp.arange(n_experts * capacity, dtype=jnp.int32)[:, None]
    selector = (
        (slot_rows[None, :, 0] == buffer_ids) | (slot_rows[None, :, 1] == buffer_ids)
    ).astype(jnp.bfloat16)
    outgoing = jnp.dot(selector, routed_in, preferred_element_type=jnp.float32).astype(jnp.bfloat16)
    outgoing = outgoing.reshape(n_experts, capacity, model_width)
    gate_local = w_gate[0]
    up_local = w_up[0]
    down_local = w_down[0]
    copies = jnp.broadcast_to(outgoing[None], (ctx_count, n_experts, capacity, model_width))
    arrived = token_move(copies.reshape(ctx_count * n_experts, capacity, model_width))
    token_rows = arrived.reshape(-1, model_width)
    gate_val = jnp.dot(token_rows, gate_local, preferred_element_type=jnp.float32)
    up_val = jnp.dot(token_rows, up_local, preferred_element_type=jnp.float32)
    slice_hidden = (jax.nn.silu(gate_val) * up_val).astype(jnp.bfloat16)
    slice_part = (
        jnp.dot(slice_hidden, down_local, preferred_element_type=jnp.float32)
        .astype(jnp.bfloat16)
        .reshape(ctx_count * n_experts, capacity, model_width)
    )
    came_back = token_move(slice_part)
    summed = jnp.sum(
        came_back.reshape(ctx_count, n_experts, capacity, model_width).astype(jnp.float32), axis=0
    )
    expert_out = stored(summed)
    flat_out = expert_out.reshape(n_experts * capacity, model_width)
    first_rows = jnp.take(flat_out, slot_rows[:, 0], axis=0).astype(jnp.float32)
    second_rows = jnp.take(flat_out, slot_rows[:, 1], axis=0).astype(jnp.float32)
    combined = weights[:, 0:1] * first_rows + weights[:, 1:2] * second_rows
    block_final = stored(hidden_state.astype(jnp.float32) + combined)
    usage_prob = jax.nn.sigmoid(
        jnp.einsum("td,od->to", block_final, splice_head, preferred_element_type=jnp.float32)
    )
    all_tokens = lax.axis_size("rep") * ctx_count * exp_count * own_rows
    loss_scale = 1.0 / math.sqrt(all_tokens)
    usage_grad = ((usage_prob - targets[0]) * loss_scale).astype(jnp.bfloat16)
    local_grad = jnp.einsum(
        "td,to->do", block_final, usage_grad, preferred_element_type=jnp.float32
    )
    head_total = a2a_allreduce(local_grad, ("ctx", "exp", "rep"), jnp.bfloat16).T
    return (block_final[None], head_total)


def solution(mesh):
    in_specs = (
        P("rep", "ctx", None),
        P(),
        P(None, None, "exp"),
        P("ctx", "exp"),
        P("exp"),
        P("exp"),
        P("exp", None),
        P(),
        P(),
        P("exp", None, "ctx"),
        P("exp", None, "ctx"),
        P("exp", "ctx", None),
        P("rep", ("ctx", "exp"), None),
        P("rep", ("ctx", "exp"), None),
        P(),
        P("rep", ("ctx", "exp"), None),
    )
    out_specs = (P("rep", ("ctx", "exp"), None), P())
    return jax.shard_map(shards, mesh=mesh, in_specs=in_specs, out_specs=out_specs, check_vma=False)
```

```python
import math

import jax
import jax.numpy as jnp
from jax import lax
from jax.sharding import PartitionSpec as P

TWO_PI = 2.0 * math.pi


def stored(values):
    return lax.optimization_barrier(values.astype(jnp.bfloat16))


def rms_scale(token_rows, norm_gain):
    wide = token_rows.astype(jnp.float32)
    inverse = lax.rsqrt(jnp.mean(wide * wide, axis=-1, keepdims=True) + 1e-05)
    return (wide * inverse * norm_gain).astype(jnp.bfloat16)


def phase_table(first_ids, second_ids, modulus):
    angle = (
        TWO_PI * (first_ids[:, None] * second_ids[None, :] % modulus).astype(jnp.float32) / modulus
    )
    return (jnp.cos(angle), jnp.sin(angle))


def spectra_move(blocks):
    return lax.all_to_all(blocks, "ctx", split_axis=0, concat_axis=1, tiled=True)


def a2a_reduce(values, axes, wire=None):
    count = lax.axis_size(axes)
    sent = values.reshape((count, -1) + values.shape[1:])
    if wire is not None:
        sent = sent.astype(wire)
    pieces = lax.all_to_all(sent, axes, 0, 0, tiled=True)
    return jnp.sum(pieces.astype(jnp.float32), axis=0)


def a2a_allreduce(values, axes, wire=None):
    count = lax.axis_size(axes)
    if values.shape[0] % count:
        return lax.psum(values, axes)
    mine = a2a_reduce(values, axes, wire)
    if wire is not None:
        mine = mine.astype(wire)
    spread = jnp.broadcast_to(mine[None], (count,) + mine.shape)
    gathered = lax.all_to_all(spread, axes, 0, 0, tiled=True)
    return gathered.astype(jnp.float32).reshape(values.shape)


def token_move(blocks):
    return lax.all_to_all(blocks, ("ctx", "exp"), split_axis=0, concat_axis=0, tiled=True)


def local_convolve(signal, kernel):
    highest = lax.Precision.HIGHEST
    lanes, length = signal.shape
    points = 2 * length
    outer = int(round(math.sqrt(points)))
    while points % outer:
        outer -= 1
    inner = points // outer
    half = length // inner
    rows = jnp.concatenate([signal, kernel], axis=0).reshape(2 * lanes, half, inner)
    a_ids = jnp.arange(half, dtype=jnp.int32)
    k1_ids = jnp.arange(outer, dtype=jnp.int32)
    b_ids = jnp.arange(inner, dtype=jnp.int32)
    k2_ids = jnp.arange(points // inner, dtype=jnp.int32)
    cos_first, sin_first = phase_table(a_ids, k1_ids, outer)
    cos_twist, sin_twist = phase_table(k1_ids, b_ids, points)
    cos_last, sin_last = phase_table(b_ids, k2_ids, inner)
    a_re = jnp.einsum("cab,ak->ckb", rows, cos_first, precision=highest)
    a_im = -jnp.einsum("cab,ak->ckb", rows, sin_first, precision=highest)
    b_re = a_re * cos_twist + a_im * sin_twist
    b_im = a_im * cos_twist - a_re * sin_twist
    x_re = jnp.einsum("ckb,bj->ckj", b_re, cos_last, precision=highest) + jnp.einsum(
        "ckb,bj->ckj", b_im, sin_last, precision=highest
    )
    x_im = jnp.einsum("ckb,bj->ckj", b_im, cos_last, precision=highest) - jnp.einsum(
        "ckb,bj->ckj", b_re, sin_last, precision=highest
    )
    p_re = x_re[:lanes] * x_re[lanes:] - x_im[:lanes] * x_im[lanes:]
    p_im = x_re[:lanes] * x_im[lanes:] + x_im[:lanes] * x_re[lanes:]
    c_re = jnp.einsum("ckj,mj->ckm", p_re, cos_last, precision=highest) - jnp.einsum(
        "ckj,mj->ckm", p_im, sin_last, precision=highest
    )
    c_im = jnp.einsum("ckj,mj->ckm", p_im, cos_last, precision=highest) + jnp.einsum(
        "ckj,mj->ckm", p_re, sin_last, precision=highest
    )
    d_re = c_re * cos_twist - c_im * sin_twist
    d_im = c_im * cos_twist + c_re * sin_twist
    out = jnp.einsum("ckm,lk->clm", d_re, cos_first, precision=highest) - jnp.einsum(
        "ckm,lk->clm", d_im, sin_first, precision=highest
    )
    return out.reshape(lanes, length) / points


def causal_convolve(source, shaped):
    both = jnp.stack([source.T, shaped.T], axis=0)
    whole = lax.all_to_all(both, "ctx", split_axis=1, concat_axis=2, tiled=True)
    convolved = local_convolve(whole[0], whole[1])
    back = lax.all_to_all(convolved, "ctx", split_axis=1, concat_axis=0, tiled=True)
    return back.T


def shards(
    sequence,
    norm1_gain,
    w_in,
    long_filter,
    filter_decay,
    conv_bias,
    w_out,
    norm2_gain,
    router,
    w_gate,
    w_up,
    w_down,
    experts,
    expert_slots,
    splice_head,
    targets,
):
    exp_count = lax.axis_size("exp")
    exp_pos = lax.axis_index("exp")
    ctx_count = lax.axis_size("ctx")
    ctx_pos = lax.axis_index("ctx")
    local_x = sequence[0]
    local_rows, model_width = local_x.shape
    own_rows = local_rows // exp_count
    length = local_rows * ctx_count
    normed = rms_scale(local_x, norm1_gain)
    projected = jnp.einsum("ti,igd->tgd", normed, w_in, preferred_element_type=jnp.float32)
    source = projected[:, 1] * projected[:, 0]
    positions = (ctx_pos * local_rows + jnp.arange(local_rows, dtype=jnp.int32)).astype(jnp.float32)
    shaped = long_filter * jnp.exp(-filter_decay[None, :] * positions[:, None] / length)
    convolved = causal_convolve(source, shaped)
    gated_rows = (projected[:, 2] * (convolved + conv_bias[None, :] * source)).astype(jnp.bfloat16)
    mixed_full = jnp.dot(gated_rows, w_out, preferred_element_type=jnp.float32)
    mixed_sum = a2a_reduce(mixed_full, "exp")
    residual_rows = lax.dynamic_slice_in_dim(local_x, exp_pos * own_rows, own_rows, 0)
    hidden_state = stored(residual_rows.astype(jnp.float32) + mixed_sum)
    routed_in = rms_scale(hidden_state, norm2_gain)
    chances = jax.nn.sigmoid(jnp.dot(routed_in, router, preferred_element_type=jnp.float32))
    picked_ids = experts[0]
    slot_ids = expert_slots[0]
    chosen = jnp.take_along_axis(chances, picked_ids, axis=1)
    weights = chosen / jnp.sum(chosen, axis=1, keepdims=True)
    n_experts = router.shape[1]
    capacity = 4 * own_rows // exp_count
    slot_rows = picked_ids * capacity + slot_ids
    buffer_ids = jnp.arange(n_experts * capacity, dtype=jnp.int32)[:, None]
    selector = (
        (slot_rows[None, :, 0] == buffer_ids) | (slot_rows[None, :, 1] == buffer_ids)
    ).astype(jnp.bfloat16)
    outgoing = jnp.dot(selector, routed_in, preferred_element_type=jnp.float32).astype(jnp.bfloat16)
    outgoing = outgoing.reshape(n_experts, capacity, model_width)
    gate_local = w_gate[0]
    up_local = w_up[0]
    down_local = w_down[0]
    copies = jnp.broadcast_to(outgoing[None], (ctx_count, n_experts, capacity, model_width))
    arrived = token_move(copies.reshape(ctx_count * n_experts, capacity, model_width))
    token_rows = arrived.reshape(-1, model_width)
    gate_val = jnp.dot(token_rows, gate_local, preferred_element_type=jnp.float32)
    up_val = jnp.dot(token_rows, up_local, preferred_element_type=jnp.float32)
    slice_hidden = (jax.nn.silu(gate_val) * up_val).astype(jnp.bfloat16)
    slice_part = (
        jnp.dot(slice_hidden, down_local, preferred_element_type=jnp.float32)
        .astype(jnp.bfloat16)
        .reshape(ctx_count * n_experts, capacity, model_width)
    )
    came_back = token_move(slice_part)
    summed = jnp.sum(
        came_back.reshape(ctx_count, n_experts, capacity, model_width).astype(jnp.float32), axis=0
    )
    expert_out = stored(summed)
    flat_out = expert_out.reshape(n_experts * capacity, model_width)
    first_rows = jnp.take(flat_out, slot_rows[:, 0], axis=0).astype(jnp.float32)
    second_rows = jnp.take(flat_out, slot_rows[:, 1], axis=0).astype(jnp.float32)
    combined = weights[:, 0:1] * first_rows + weights[:, 1:2] * second_rows
    block_final = stored(hidden_state.astype(jnp.float32) + combined)
    usage_prob = jax.nn.sigmoid(
        jnp.einsum("td,od->to", block_final, splice_head, preferred_element_type=jnp.float32)
    )
    all_tokens = lax.axis_size("rep") * ctx_count * exp_count * own_rows
    loss_scale = 1.0 / math.sqrt(all_tokens)
    usage_grad = ((usage_prob - targets[0]) * loss_scale).astype(jnp.bfloat16)
    local_grad = jnp.einsum(
        "td,to->do", block_final, usage_grad, preferred_element_type=jnp.float32
    )
    head_total = a2a_allreduce(local_grad, ("ctx", "exp", "rep"), jnp.bfloat16).T
    return (block_final[None], head_total)


def solution(mesh):
    in_specs = (
        P("rep", "ctx", None),
        P(),
        P(None, None, "exp"),
        P("ctx", "exp"),
        P("exp"),
        P("exp"),
        P("exp", None),
        P(),
        P(),
        P("exp", None, "ctx"),
        P("exp", None, "ctx"),
        P("exp", "ctx", None),
        P("rep", ("ctx", "exp"), None),
        P("rep", ("ctx", "exp"), None),
        P(),
        P("rep", ("ctx", "exp"), None),
    )
    out_specs = (P("rep", ("ctx", "exp"), None), P())
    return jax.shard_map(shards, mesh=mesh, in_specs=in_specs, out_specs=out_specs, check_vma=False)
```

```python
import math

import jax
import jax.numpy as jnp
from jax import lax
from jax.sharding import PartitionSpec as P

TWO_PI = 2.0 * math.pi


def stored(values):
    return lax.optimization_barrier(values.astype(jnp.bfloat16))


def rms_scale(token_rows, norm_gain):
    wide = token_rows.astype(jnp.float32)
    inverse = lax.rsqrt(jnp.mean(wide * wide, axis=-1, keepdims=True) + 1e-05)
    return (wide * inverse * norm_gain).astype(jnp.bfloat16)


def phase_table(first_ids, second_ids, modulus):
    angle = (
        TWO_PI * (first_ids[:, None] * second_ids[None, :] % modulus).astype(jnp.float32) / modulus
    )
    return (jnp.cos(angle), jnp.sin(angle))


def spectra_move(blocks):
    return lax.all_to_all(blocks, "ctx", split_axis=0, concat_axis=1, tiled=True)


def a2a_reduce(values, axes, wire=None):
    count = lax.axis_size(axes)
    sent = values.reshape((count, -1) + values.shape[1:])
    if wire is not None:
        sent = sent.astype(wire)
    pieces = lax.all_to_all(sent, axes, 0, 0, tiled=True)
    return jnp.sum(pieces.astype(jnp.float32), axis=0)


def a2a_allreduce(values, axes, wire=None):
    count = lax.axis_size(axes)
    if values.shape[0] % count:
        return lax.psum(values, axes)
    mine = a2a_reduce(values, axes, wire)
    if wire is not None:
        mine = mine.astype(wire)
    spread = jnp.broadcast_to(mine[None], (count,) + mine.shape)
    gathered = lax.all_to_all(spread, axes, 0, 0, tiled=True)
    return gathered.astype(jnp.float32).reshape(values.shape)


def token_move(blocks):
    return lax.all_to_all(blocks, ("ctx", "exp"), split_axis=0, concat_axis=0, tiled=True)


def local_spectrum(rows):
    highest = lax.Precision.HIGHEST
    lanes, length = rows.shape
    points = 2 * length
    outer = int(round(math.sqrt(points)))
    while points % outer:
        outer -= 1
    inner = points // outer
    half = length // inner
    rows = rows.reshape(lanes, half, inner)
    a_ids = jnp.arange(half, dtype=jnp.int32)
    k1_ids = jnp.arange(outer, dtype=jnp.int32)
    b_ids = jnp.arange(inner, dtype=jnp.int32)
    k2_ids = jnp.arange(points // inner, dtype=jnp.int32)
    cos_first, sin_first = phase_table(a_ids, k1_ids, outer)
    cos_twist, sin_twist = phase_table(k1_ids, b_ids, points)
    cos_last, sin_last = phase_table(b_ids, k2_ids, inner)
    a_re = jnp.einsum("cab,ak->ckb", rows, cos_first, precision=highest)
    a_im = -jnp.einsum("cab,ak->ckb", rows, sin_first, precision=highest)
    b_re = a_re * cos_twist + a_im * sin_twist
    b_im = a_im * cos_twist - a_re * sin_twist
    x_re = jnp.einsum("ckb,bj->ckj", b_re, cos_last, precision=highest) + jnp.einsum(
        "ckb,bj->ckj", b_im, sin_last, precision=highest
    )
    x_im = jnp.einsum("ckb,bj->ckj", b_im, cos_last, precision=highest) - jnp.einsum(
        "ckb,bj->ckj", b_re, sin_last, precision=highest
    )
    return x_re, x_im


def local_convolve(signal_re, signal_im, kernel_re, kernel_im, length):
    highest = lax.Precision.HIGHEST
    lanes = signal_re.shape[0]
    points = 2 * length
    outer = int(round(math.sqrt(points)))
    while points % outer:
        outer -= 1
    inner = points // outer
    half = length // inner
    a_ids = jnp.arange(half, dtype=jnp.int32)
    k1_ids = jnp.arange(outer, dtype=jnp.int32)
    b_ids = jnp.arange(inner, dtype=jnp.int32)
    k2_ids = jnp.arange(points // inner, dtype=jnp.int32)
    cos_first, sin_first = phase_table(a_ids, k1_ids, outer)
    cos_twist, sin_twist = phase_table(k1_ids, b_ids, points)
    cos_last, sin_last = phase_table(b_ids, k2_ids, inner)
    p_re = signal_re * kernel_re - signal_im * kernel_im
    p_im = signal_re * kernel_im + signal_im * kernel_re
    c_re = jnp.einsum("ckj,mj->ckm", p_re, cos_last, precision=highest) - jnp.einsum(
        "ckj,mj->ckm", p_im, sin_last, precision=highest
    )
    c_im = jnp.einsum("ckj,mj->ckm", p_im, cos_last, precision=highest) + jnp.einsum(
        "ckj,mj->ckm", p_re, sin_last, precision=highest
    )
    d_re = c_re * cos_twist - c_im * sin_twist
    d_im = c_im * cos_twist + c_re * sin_twist
    out = jnp.einsum("ckm,lk->clm", d_re, cos_first, precision=highest) - jnp.einsum(
        "ckm,lk->clm", d_im, sin_first, precision=highest
    )
    return out.reshape(lanes, length) / points


def to_sequences(rows):
    return lax.all_to_all(rows.T, "ctx", split_axis=0, concat_axis=1, tiled=True)


def causal_convolve(source, kernel_re, kernel_im):
    whole = to_sequences(source)
    signal_re, signal_im = local_spectrum(whole)
    convolved = local_convolve(signal_re, signal_im, kernel_re, kernel_im, whole.shape[1])
    back = lax.all_to_all(convolved, "ctx", split_axis=1, concat_axis=0, tiled=True)
    return back.T


def shards(
    sequence,
    norm1_gain,
    w_in,
    long_filter,
    filter_decay,
    conv_bias,
    w_out,
    norm2_gain,
    router,
    w_gate,
    w_up,
    w_down,
    experts,
    expert_slots,
    splice_head,
    targets,
):
    exp_count = lax.axis_size("exp")
    exp_pos = lax.axis_index("exp")
    ctx_count = lax.axis_size("ctx")
    ctx_pos = lax.axis_index("ctx")
    local_x = sequence[0]
    local_rows, model_width = local_x.shape
    own_rows = local_rows // exp_count
    length = local_rows * ctx_count
    positions = (ctx_pos * local_rows + jnp.arange(local_rows, dtype=jnp.int32)).astype(jnp.float32)
    shaped = long_filter * jnp.exp(-filter_decay[None, :] * positions[:, None] / length)
    kernel_re, kernel_im = local_spectrum(to_sequences(shaped))
    normed = rms_scale(local_x, norm1_gain)
    projected = jnp.einsum("ti,igd->tgd", normed, w_in, preferred_element_type=jnp.float32)
    source = projected[:, 1] * projected[:, 0]
    convolved = causal_convolve(source, kernel_re, kernel_im)
    gated_rows = (projected[:, 2] * (convolved + conv_bias[None, :] * source)).astype(jnp.bfloat16)
    mixed_full = jnp.dot(gated_rows, w_out, preferred_element_type=jnp.float32)
    mixed_sum = a2a_reduce(mixed_full, "exp", jnp.bfloat16)
    residual_rows = lax.dynamic_slice_in_dim(local_x, exp_pos * own_rows, own_rows, 0)
    hidden_state = stored(residual_rows.astype(jnp.float32) + mixed_sum)
    routed_in = rms_scale(hidden_state, norm2_gain)
    chances = jax.nn.sigmoid(jnp.dot(routed_in, router, preferred_element_type=jnp.float32))
    picked_ids = experts[0]
    slot_ids = expert_slots[0]
    chosen = jnp.take_along_axis(chances, picked_ids, axis=1)
    weights = chosen / jnp.sum(chosen, axis=1, keepdims=True)
    n_experts = router.shape[1]
    capacity = 4 * own_rows // exp_count
    slot_rows = picked_ids * capacity + slot_ids
    buffer_ids = jnp.arange(n_experts * capacity, dtype=jnp.int32)[:, None]
    selector = (
        (slot_rows[None, :, 0] == buffer_ids) | (slot_rows[None, :, 1] == buffer_ids)
    ).astype(jnp.bfloat16)
    outgoing = jnp.dot(selector, routed_in, preferred_element_type=jnp.float32).astype(jnp.bfloat16)
    outgoing = outgoing.reshape(n_experts, capacity, model_width)
    gate_local = w_gate[0]
    up_local = w_up[0]
    down_local = w_down[0]
    copies = jnp.broadcast_to(outgoing[None], (ctx_count, n_experts, capacity, model_width))
    arrived = token_move(copies.reshape(ctx_count * n_experts, capacity, model_width))
    token_rows = arrived.reshape(-1, model_width)
    gate_val = jnp.dot(token_rows, gate_local, preferred_element_type=jnp.float32)
    up_val = jnp.dot(token_rows, up_local, preferred_element_type=jnp.float32)
    slice_hidden = (jax.nn.silu(gate_val) * up_val).astype(jnp.bfloat16)
    slice_part = (
        jnp.dot(slice_hidden, down_local, preferred_element_type=jnp.float32)
        .astype(jnp.bfloat16)
        .reshape(ctx_count * n_experts, capacity, model_width)
    )
    came_back = token_move(slice_part)
    summed = jnp.sum(
        came_back.reshape(ctx_count, n_experts, capacity, model_width).astype(jnp.float32), axis=0
    )
    expert_out = stored(summed)
    flat_out = expert_out.reshape(n_experts * capacity, model_width)
    first_rows = jnp.take(flat_out, slot_rows[:, 0], axis=0).astype(jnp.float32)
    second_rows = jnp.take(flat_out, slot_rows[:, 1], axis=0).astype(jnp.float32)
    combined = weights[:, 0:1] * first_rows + weights[:, 1:2] * second_rows
    block_final = stored(hidden_state.astype(jnp.float32) + combined)
    usage_prob = jax.nn.sigmoid(
        jnp.einsum("td,od->to", block_final, splice_head, preferred_element_type=jnp.float32)
    )
    all_tokens = lax.axis_size("rep") * ctx_count * exp_count * own_rows
    loss_scale = 1.0 / math.sqrt(all_tokens)
    usage_grad = ((usage_prob - targets[0]) * loss_scale).astype(jnp.bfloat16)
    local_grad = jnp.einsum(
        "td,to->do", block_final, usage_grad, preferred_element_type=jnp.float32
    )
    head_total = a2a_allreduce(local_grad, ("ctx", "exp", "rep"), jnp.bfloat16).T
    return (block_final[None], head_total)


def solution(mesh):
    in_specs = (
        P("rep", "ctx", None),
        P(),
        P(None, None, "exp"),
        P("ctx", "exp"),
        P("exp"),
        P("exp"),
        P("exp", None),
        P(),
        P(),
        P("exp", None, "ctx"),
        P("exp", None, "ctx"),
        P("exp", "ctx", None),
        P("rep", ("ctx", "exp"), None),
        P("rep", ("ctx", "exp"), None),
        P(),
        P("rep", ("ctx", "exp"), None),
    )
    out_specs = (P("rep", ("ctx", "exp"), None), P())
    return jax.shard_map(shards, mesh=mesh, in_specs=in_specs, out_specs=out_specs, check_vma=False)
```

```python
import math

import jax
import jax.numpy as jnp
from jax import lax
from jax.sharding import PartitionSpec as P

TWO_PI = 2.0 * math.pi


def stored(values):
    return lax.optimization_barrier(values.astype(jnp.bfloat16))


def rms_scale(token_rows, norm_gain):
    wide = token_rows.astype(jnp.float32)
    inverse = lax.rsqrt(jnp.mean(wide * wide, axis=-1, keepdims=True) + 1e-05)
    return (wide * inverse * norm_gain).astype(jnp.bfloat16)


def phase_table(first_ids, second_ids, modulus):
    angle = (
        TWO_PI * (first_ids[:, None] * second_ids[None, :] % modulus).astype(jnp.float32) / modulus
    )
    return (jnp.cos(angle), jnp.sin(angle))


def spectra_move(blocks):
    return lax.all_to_all(blocks, "ctx", split_axis=0, concat_axis=1, tiled=True)


def a2a_reduce(values, axes, wire=None):
    count = lax.axis_size(axes)
    sent = values.reshape((count, -1) + values.shape[1:])
    if wire is not None:
        sent = sent.astype(wire)
    pieces = lax.all_to_all(sent, axes, 0, 0, tiled=True)
    return jnp.sum(pieces.astype(jnp.float32), axis=0)


def a2a_allreduce(values, axes, wire=None):
    count = lax.axis_size(axes)
    if values.shape[0] % count:
        return lax.psum(values, axes)
    mine = a2a_reduce(values, axes, wire)
    if wire is not None:
        mine = mine.astype(wire)
    spread = jnp.broadcast_to(mine[None], (count,) + mine.shape)
    gathered = lax.all_to_all(spread, axes, 0, 0, tiled=True)
    return gathered.astype(jnp.float32).reshape(values.shape)


def token_move(blocks):
    return lax.all_to_all(blocks, ("ctx", "exp"), split_axis=0, concat_axis=0, tiled=True)


def local_convolve(signal, kernel):
    highest = lax.Precision.HIGHEST
    lanes, length = signal.shape
    points = 2 * length
    outer = int(round(math.sqrt(points)))
    while points % outer:
        outer -= 1
    inner = points // outer
    half = length // inner
    rows = jnp.concatenate([signal, kernel], axis=0).reshape(2 * lanes, half, inner)
    a_ids = jnp.arange(half, dtype=jnp.int32)
    k1_ids = jnp.arange(outer, dtype=jnp.int32)
    b_ids = jnp.arange(inner, dtype=jnp.int32)
    k2_ids = jnp.arange(points // inner, dtype=jnp.int32)
    cos_first, sin_first = phase_table(a_ids, k1_ids, outer)
    cos_twist, sin_twist = phase_table(k1_ids, b_ids, points)
    cos_last, sin_last = phase_table(b_ids, k2_ids, inner)
    a_re = jnp.einsum("cab,ak->ckb", rows, cos_first, precision=highest)
    a_im = -jnp.einsum("cab,ak->ckb", rows, sin_first, precision=highest)
    b_re = a_re * cos_twist + a_im * sin_twist
    b_im = a_im * cos_twist - a_re * sin_twist
    x_re = jnp.einsum("ckb,bj->ckj", b_re, cos_last, precision=highest) + jnp.einsum(
        "ckb,bj->ckj", b_im, sin_last, precision=highest
    )
    x_im = jnp.einsum("ckb,bj->ckj", b_im, cos_last, precision=highest) - jnp.einsum(
        "ckb,bj->ckj", b_re, sin_last, precision=highest
    )
    p_re = x_re[:lanes] * x_re[lanes:] - x_im[:lanes] * x_im[lanes:]
    p_im = x_re[:lanes] * x_im[lanes:] + x_im[:lanes] * x_re[lanes:]
    c_re = jnp.einsum("ckj,mj->ckm", p_re, cos_last, precision=highest) - jnp.einsum(
        "ckj,mj->ckm", p_im, sin_last, precision=highest
    )
    c_im = jnp.einsum("ckj,mj->ckm", p_im, cos_last, precision=highest) + jnp.einsum(
        "ckj,mj->ckm", p_re, sin_last, precision=highest
    )
    d_re = c_re * cos_twist - c_im * sin_twist
    d_im = c_im * cos_twist + c_re * sin_twist
    out = jnp.einsum("ckm,lk->clm", d_re, cos_first, precision=highest) - jnp.einsum(
        "ckm,lk->clm", d_im, sin_first, precision=highest
    )
    return out.reshape(lanes, length) / points


def causal_convolve(source, shaped):
    both = jnp.stack([source.T, shaped.T], axis=0)
    whole = lax.all_to_all(both, "ctx", split_axis=1, concat_axis=2, tiled=True)
    convolved = local_convolve(whole[0], whole[1])
    back = lax.all_to_all(convolved, "ctx", split_axis=1, concat_axis=0, tiled=True)
    return back.T


def shards(
    sequence,
    norm1_gain,
    w_in,
    long_filter,
    filter_decay,
    conv_bias,
    w_out,
    norm2_gain,
    router,
    w_gate,
    w_up,
    w_down,
    experts,
    expert_slots,
    splice_head,
    targets,
):
    exp_count = lax.axis_size("exp")
    exp_pos = lax.axis_index("exp")
    ctx_count = lax.axis_size("ctx")
    ctx_pos = lax.axis_index("ctx")
    local_x = sequence[0]
    local_rows, model_width = local_x.shape
    own_rows = local_rows // exp_count
    length = local_rows * ctx_count
    normed = rms_scale(local_x, norm1_gain)
    projected = jnp.einsum("ti,igd->tgd", normed, w_in, preferred_element_type=jnp.float32)
    source = projected[:, 1] * projected[:, 0]
    positions = (ctx_pos * local_rows + jnp.arange(local_rows, dtype=jnp.int32)).astype(jnp.float32)
    shaped = long_filter * jnp.exp(-filter_decay[None, :] * positions[:, None] / length)
    convolved = causal_convolve(source, shaped)
    gated_rows = (projected[:, 2] * (convolved + conv_bias[None, :] * source)).astype(jnp.bfloat16)
    mixed_full = jnp.dot(gated_rows, w_out, preferred_element_type=jnp.float32)
    mixed_sum = a2a_reduce(mixed_full, "exp", jnp.bfloat16)
    residual_rows = lax.dynamic_slice_in_dim(local_x, exp_pos * own_rows, own_rows, 0)
    hidden_state = stored(residual_rows.astype(jnp.float32) + mixed_sum)
    routed_in = rms_scale(hidden_state, norm2_gain)
    chances = jax.nn.sigmoid(jnp.dot(routed_in, router, preferred_element_type=jnp.float32))
    picked_ids = experts[0]
    slot_ids = expert_slots[0]
    chosen = jnp.take_along_axis(chances, picked_ids, axis=1)
    weights = chosen / jnp.sum(chosen, axis=1, keepdims=True)
    n_experts = router.shape[1]
    capacity = 4 * own_rows // exp_count
    slot_rows = picked_ids * capacity + slot_ids
    buffer_ids = jnp.arange(n_experts * capacity, dtype=jnp.int32)[:, None]
    selector = (
        (slot_rows[None, :, 0] == buffer_ids) | (slot_rows[None, :, 1] == buffer_ids)
    ).astype(jnp.bfloat16)
    outgoing = jnp.dot(selector, routed_in, preferred_element_type=jnp.float32).astype(jnp.bfloat16)
    outgoing = outgoing.reshape(n_experts, capacity, model_width)
    gate_local = w_gate[0]
    up_local = w_up[0]
    down_local = w_down[0]
    copies = jnp.broadcast_to(outgoing[None], (ctx_count, n_experts, capacity, model_width))
    arrived = token_move(copies.reshape(ctx_count * n_experts, capacity, model_width))
    token_rows = arrived.reshape(-1, model_width)
    gate_val = jnp.dot(token_rows, gate_local, preferred_element_type=jnp.float32)
    up_val = jnp.dot(token_rows, up_local, preferred_element_type=jnp.float32)
    slice_hidden = lax.optimization_barrier((jax.nn.silu(gate_val) * up_val).astype(jnp.bfloat16))
    slice_part = (
        jnp.dot(slice_hidden, down_local, preferred_element_type=jnp.float32)
        .astype(jnp.bfloat16)
        .reshape(ctx_count * n_experts, capacity, model_width)
    )
    came_back = token_move(slice_part)
    summed = jnp.sum(
        came_back.reshape(ctx_count, n_experts, capacity, model_width).astype(jnp.float32), axis=0
    )
    expert_out = stored(summed)
    flat_out = expert_out.reshape(n_experts * capacity, model_width)
    first_rows = jnp.take(flat_out, slot_rows[:, 0], axis=0).astype(jnp.float32)
    second_rows = jnp.take(flat_out, slot_rows[:, 1], axis=0).astype(jnp.float32)
    combined = weights[:, 0:1] * first_rows + weights[:, 1:2] * second_rows
    block_final = stored(hidden_state.astype(jnp.float32) + combined)
    usage_prob = jax.nn.sigmoid(
        jnp.einsum("td,od->to", block_final, splice_head, preferred_element_type=jnp.float32)
    )
    all_tokens = lax.axis_size("rep") * ctx_count * exp_count * own_rows
    loss_scale = 1.0 / math.sqrt(all_tokens)
    usage_grad = ((usage_prob - targets[0]) * loss_scale).astype(jnp.bfloat16)
    local_grad = jnp.einsum(
        "td,to->do", block_final, usage_grad, preferred_element_type=jnp.float32
    )
    head_total = a2a_allreduce(local_grad, ("ctx", "exp", "rep"), jnp.bfloat16).T
    return (block_final[None], head_total)


def solution(mesh):
    in_specs = (
        P("rep", "ctx", None),
        P(),
        P(None, None, "exp"),
        P("ctx", "exp"),
        P("exp"),
        P("exp"),
        P("exp", None),
        P(),
        P(),
        P("exp", None, "ctx"),
        P("exp", None, "ctx"),
        P("exp", "ctx", None),
        P("rep", ("ctx", "exp"), None),
        P("rep", ("ctx", "exp"), None),
        P(),
        P("rep", ("ctx", "exp"), None),
    )
    out_specs = (P("rep", ("ctx", "exp"), None), P())
    return jax.shard_map(shards, mesh=mesh, in_specs=in_specs, out_specs=out_specs, check_vma=False)
```

```python
import math

import jax
import jax.numpy as jnp
from jax import lax
from jax.sharding import PartitionSpec as P

TWO_PI = 2.0 * math.pi


def stored(values):
    return lax.optimization_barrier(values.astype(jnp.bfloat16))


def rms_scale(token_rows, norm_gain):
    wide = token_rows.astype(jnp.float32)
    inverse = lax.rsqrt(jnp.mean(wide * wide, axis=-1, keepdims=True) + 1e-05)
    return (wide * inverse * norm_gain).astype(jnp.bfloat16)


def phase_table(first_ids, second_ids, modulus):
    angle = (
        TWO_PI * (first_ids[:, None] * second_ids[None, :] % modulus).astype(jnp.float32) / modulus
    )
    return (jnp.cos(angle), jnp.sin(angle))


def spectra_move(blocks):
    return lax.all_to_all(blocks, "ctx", split_axis=0, concat_axis=1, tiled=True)


def a2a_reduce(values, axes, wire=None):
    count = lax.axis_size(axes)
    sent = values.reshape((count, -1) + values.shape[1:])
    if wire is not None:
        sent = sent.astype(wire)
    pieces = lax.all_to_all(sent, axes, 0, 0, tiled=True)
    return jnp.sum(pieces.astype(jnp.float32), axis=0)


def a2a_allreduce(values, axes, wire=None):
    count = lax.axis_size(axes)
    if values.shape[0] % count:
        return lax.psum(values, axes)
    mine = a2a_reduce(values, axes, wire)
    if wire is not None:
        mine = mine.astype(wire)
    spread = jnp.broadcast_to(mine[None], (count,) + mine.shape)
    gathered = lax.all_to_all(spread, axes, 0, 0, tiled=True)
    return gathered.astype(jnp.float32).reshape(values.shape)


def token_move(blocks):
    return lax.all_to_all(blocks, ("ctx", "exp"), split_axis=0, concat_axis=0, tiled=True)


def local_convolve(signal, kernel):
    highest = lax.Precision.HIGHEST
    lanes, length = signal.shape
    points = 2 * length
    outer = int(round(math.sqrt(points)))
    while points % outer:
        outer -= 1
    inner = points // outer
    half = length // inner
    rows = jnp.concatenate([signal, kernel], axis=0).reshape(2 * lanes, half, inner)
    a_ids = jnp.arange(half, dtype=jnp.int32)
    k1_ids = jnp.arange(outer, dtype=jnp.int32)
    b_ids = jnp.arange(inner, dtype=jnp.int32)
    k2_ids = jnp.arange(points // inner, dtype=jnp.int32)
    cos_first, sin_first = phase_table(a_ids, k1_ids, outer)
    cos_twist, sin_twist = phase_table(k1_ids, b_ids, points)
    cos_last, sin_last = phase_table(b_ids, k2_ids, inner)
    first = jnp.stack([cos_first, -sin_first], axis=1)
    spread = jnp.einsum("cab,azk->czkb", rows, first, precision=highest)
    twisted = jnp.stack(
        [
            spread[:, 0] * cos_twist + spread[:, 1] * sin_twist,
            spread[:, 1] * cos_twist - spread[:, 0] * sin_twist,
        ],
        axis=1,
    )
    forward = jnp.stack(
        [jnp.stack([cos_last, -sin_last], axis=1), jnp.stack([sin_last, cos_last], axis=1)], axis=0
    )
    spectra = jnp.einsum("czkb,zbwj->cwkj", twisted, forward, precision=highest)
    sig, ker = spectra[:lanes], spectra[lanes:]
    product = jnp.stack(
        [
            sig[:, 0] * ker[:, 0] - sig[:, 1] * ker[:, 1],
            sig[:, 0] * ker[:, 1] + sig[:, 1] * ker[:, 0],
        ],
        axis=1,
    )
    backward = jnp.stack(
        [jnp.stack([cos_last, sin_last], axis=1), jnp.stack([-sin_last, cos_last], axis=1)], axis=0
    )
    partial = jnp.einsum("czkj,zjwm->cwkm", product, backward, precision=highest)
    untwisted = jnp.stack(
        [
            partial[:, 0] * cos_twist - partial[:, 1] * sin_twist,
            partial[:, 1] * cos_twist + partial[:, 0] * sin_twist,
        ],
        axis=1,
    )
    last = jnp.stack([cos_first, -sin_first], axis=0)
    out = jnp.einsum("czkm,zlk->clm", untwisted, last, precision=highest)
    return out.reshape(lanes, length) / points


def causal_convolve(source, shaped):
    both = jnp.stack([source.T, shaped.T], axis=0)
    whole = lax.all_to_all(both, "ctx", split_axis=1, concat_axis=2, tiled=True)
    convolved = local_convolve(whole[0], whole[1])
    back = lax.all_to_all(convolved, "ctx", split_axis=1, concat_axis=0, tiled=True)
    return back.T


def shards(
    sequence,
    norm1_gain,
    w_in,
    long_filter,
    filter_decay,
    conv_bias,
    w_out,
    norm2_gain,
    router,
    w_gate,
    w_up,
    w_down,
    experts,
    expert_slots,
    splice_head,
    targets,
):
    exp_count = lax.axis_size("exp")
    exp_pos = lax.axis_index("exp")
    ctx_count = lax.axis_size("ctx")
    ctx_pos = lax.axis_index("ctx")
    local_x = sequence[0]
    local_rows, model_width = local_x.shape
    own_rows = local_rows // exp_count
    length = local_rows * ctx_count
    normed = rms_scale(local_x, norm1_gain)
    projected = jnp.einsum("ti,igd->tgd", normed, w_in, preferred_element_type=jnp.float32)
    source = projected[:, 1] * projected[:, 0]
    positions = (ctx_pos * local_rows + jnp.arange(local_rows, dtype=jnp.int32)).astype(jnp.float32)
    shaped = long_filter * jnp.exp(-filter_decay[None, :] * positions[:, None] / length)
    convolved = causal_convolve(source, shaped)
    gated_rows = (projected[:, 2] * (convolved + conv_bias[None, :] * source)).astype(jnp.bfloat16)
    mixed_full = jnp.dot(gated_rows, w_out, preferred_element_type=jnp.float32)
    mixed_sum = a2a_reduce(mixed_full, "exp", jnp.bfloat16)
    residual_rows = lax.dynamic_slice_in_dim(local_x, exp_pos * own_rows, own_rows, 0)
    hidden_state = stored(residual_rows.astype(jnp.float32) + mixed_sum)
    routed_in = rms_scale(hidden_state, norm2_gain)
    chances = jax.nn.sigmoid(jnp.dot(routed_in, router, preferred_element_type=jnp.float32))
    picked_ids = experts[0]
    slot_ids = expert_slots[0]
    chosen = jnp.take_along_axis(chances, picked_ids, axis=1)
    weights = chosen / jnp.sum(chosen, axis=1, keepdims=True)
    n_experts = router.shape[1]
    capacity = 4 * own_rows // exp_count
    slot_rows = picked_ids * capacity + slot_ids
    buffer_ids = jnp.arange(n_experts * capacity, dtype=jnp.int32)[:, None]
    selector = (
        (slot_rows[None, :, 0] == buffer_ids) | (slot_rows[None, :, 1] == buffer_ids)
    ).astype(jnp.bfloat16)
    outgoing = jnp.dot(selector, routed_in, preferred_element_type=jnp.float32).astype(jnp.bfloat16)
    outgoing = outgoing.reshape(n_experts, capacity, model_width)
    gate_local = w_gate[0]
    up_local = w_up[0]
    down_local = w_down[0]
    copies = jnp.broadcast_to(outgoing[None], (ctx_count, n_experts, capacity, model_width))
    arrived = token_move(copies.reshape(ctx_count * n_experts, capacity, model_width))
    token_rows = arrived.reshape(-1, model_width)
    gate_val = jnp.dot(token_rows, gate_local, preferred_element_type=jnp.float32)
    up_val = jnp.dot(token_rows, up_local, preferred_element_type=jnp.float32)
    slice_hidden = lax.optimization_barrier((jax.nn.silu(gate_val) * up_val).astype(jnp.bfloat16))
    slice_part = (
        jnp.dot(slice_hidden, down_local, preferred_element_type=jnp.float32)
        .astype(jnp.bfloat16)
        .reshape(ctx_count * n_experts, capacity, model_width)
    )
    came_back = token_move(slice_part)
    summed = jnp.sum(
        came_back.reshape(ctx_count, n_experts, capacity, model_width).astype(jnp.float32), axis=0
    )
    expert_out = stored(summed)
    flat_out = expert_out.reshape(n_experts * capacity, model_width)
    first_rows = jnp.take(flat_out, slot_rows[:, 0], axis=0).astype(jnp.float32)
    second_rows = jnp.take(flat_out, slot_rows[:, 1], axis=0).astype(jnp.float32)
    combined = weights[:, 0:1] * first_rows + weights[:, 1:2] * second_rows
    block_final = stored(hidden_state.astype(jnp.float32) + combined)
    usage_prob = jax.nn.sigmoid(
        jnp.einsum("td,od->to", block_final, splice_head, preferred_element_type=jnp.float32)
    )
    all_tokens = lax.axis_size("rep") * ctx_count * exp_count * own_rows
    loss_scale = 1.0 / math.sqrt(all_tokens)
    usage_grad = ((usage_prob - targets[0]) * loss_scale).astype(jnp.bfloat16)
    local_grad = jnp.einsum(
        "td,to->do", block_final, usage_grad, preferred_element_type=jnp.float32
    )
    head_total = a2a_allreduce(local_grad, ("ctx", "exp", "rep"), jnp.bfloat16).T
    return (block_final[None], head_total)


def solution(mesh):
    in_specs = (
        P("rep", "ctx", None),
        P(),
        P(None, None, "exp"),
        P("ctx", "exp"),
        P("exp"),
        P("exp"),
        P("exp", None),
        P(),
        P(),
        P("exp", None, "ctx"),
        P("exp", None, "ctx"),
        P("exp", "ctx", None),
        P("rep", ("ctx", "exp"), None),
        P("rep", ("ctx", "exp"), None),
        P(),
        P("rep", ("ctx", "exp"), None),
    )
    out_specs = (P("rep", ("ctx", "exp"), None), P())
    return jax.shard_map(shards, mesh=mesh, in_specs=in_specs, out_specs=out_specs, check_vma=False)
```

```python
import math

import jax
import jax.numpy as jnp
from jax import lax
from jax.sharding import PartitionSpec as P

TWO_PI = 2.0 * math.pi


def stored(values):
    return lax.optimization_barrier(values.astype(jnp.bfloat16))


def rms_scale(token_rows, norm_gain):
    wide = token_rows.astype(jnp.float32)
    inverse = lax.rsqrt(jnp.mean(wide * wide, axis=-1, keepdims=True) + 1e-05)
    return (wide * inverse * norm_gain).astype(jnp.bfloat16)


def phase_table(first_ids, second_ids, modulus):
    angle = (
        TWO_PI * (first_ids[:, None] * second_ids[None, :] % modulus).astype(jnp.float32) / modulus
    )
    return (jnp.cos(angle), jnp.sin(angle))


def spectra_move(blocks):
    return lax.all_to_all(blocks, "ctx", split_axis=0, concat_axis=1, tiled=True)


def a2a_reduce(values, axes, wire=None):
    count = lax.axis_size(axes)
    sent = values.reshape((count, -1) + values.shape[1:])
    if wire is not None:
        sent = sent.astype(wire)
    pieces = lax.all_to_all(sent, axes, 0, 0, tiled=True)
    return jnp.sum(pieces.astype(jnp.float32), axis=0)


def a2a_allreduce(values, axes, wire=None):
    count = lax.axis_size(axes)
    if values.shape[0] % count:
        return lax.psum(values, axes)
    mine = a2a_reduce(values, axes, wire)
    if wire is not None:
        mine = mine.astype(wire)
    spread = jnp.broadcast_to(mine[None], (count,) + mine.shape)
    gathered = lax.all_to_all(spread, axes, 0, 0, tiled=True)
    return gathered.astype(jnp.float32).reshape(values.shape)


def token_move(blocks):
    return lax.all_to_all(blocks, ("ctx", "exp"), split_axis=0, concat_axis=0, tiled=True)


def local_convolve(whole):
    highest = lax.Precision.HIGHEST
    _, lanes, length = whole.shape
    points = 2 * length
    outer = int(round(math.sqrt(points)))
    while points % outer:
        outer -= 1
    inner = points // outer
    half = length // inner
    rows = whole.reshape(2 * lanes, half, inner)
    a_ids = jnp.arange(half, dtype=jnp.int32)
    k1_ids = jnp.arange(outer, dtype=jnp.int32)
    b_ids = jnp.arange(inner, dtype=jnp.int32)
    k2_ids = jnp.arange(points // inner, dtype=jnp.int32)
    cos_first, sin_first = phase_table(a_ids, k1_ids, outer)
    cos_twist, sin_twist = phase_table(k1_ids, b_ids, points)
    cos_last, sin_last = phase_table(b_ids, k2_ids, inner)
    a_re = jnp.einsum("cab,ak->ckb", rows, cos_first, precision=highest)
    a_im = -jnp.einsum("cab,ak->ckb", rows, sin_first, precision=highest)
    b_re = a_re * cos_twist + a_im * sin_twist
    b_im = a_im * cos_twist - a_re * sin_twist
    x_re = jnp.einsum("ckb,bj->ckj", b_re, cos_last, precision=highest) + jnp.einsum(
        "ckb,bj->ckj", b_im, sin_last, precision=highest
    )
    x_im = jnp.einsum("ckb,bj->ckj", b_im, cos_last, precision=highest) - jnp.einsum(
        "ckb,bj->ckj", b_re, sin_last, precision=highest
    )
    p_re = x_re[:lanes] * x_re[lanes:] - x_im[:lanes] * x_im[lanes:]
    p_im = x_re[:lanes] * x_im[lanes:] + x_im[:lanes] * x_re[lanes:]
    c_re = jnp.einsum("ckj,mj->ckm", p_re, cos_last, precision=highest) - jnp.einsum(
        "ckj,mj->ckm", p_im, sin_last, precision=highest
    )
    c_im = jnp.einsum("ckj,mj->ckm", p_im, cos_last, precision=highest) + jnp.einsum(
        "ckj,mj->ckm", p_re, sin_last, precision=highest
    )
    d_re = c_re * cos_twist - c_im * sin_twist
    d_im = c_im * cos_twist + c_re * sin_twist
    out = jnp.einsum("ckm,lk->clm", d_re, cos_first, precision=highest) - jnp.einsum(
        "ckm,lk->clm", d_im, sin_first, precision=highest
    )
    return out.reshape(lanes, length) / points


def causal_convolve(source, shaped):
    both = jnp.stack([source.T, shaped.T], axis=0)
    whole = lax.all_to_all(both, "ctx", split_axis=1, concat_axis=2, tiled=True)
    convolved = local_convolve(whole)
    back = lax.all_to_all(convolved, "ctx", split_axis=1, concat_axis=0, tiled=True)
    return back.T


def shards(
    sequence,
    norm1_gain,
    w_in,
    long_filter,
    filter_decay,
    conv_bias,
    w_out,
    norm2_gain,
    router,
    w_gate,
    w_up,
    w_down,
    experts,
    expert_slots,
    splice_head,
    targets,
):
    exp_count = lax.axis_size("exp")
    exp_pos = lax.axis_index("exp")
    ctx_count = lax.axis_size("ctx")
    ctx_pos = lax.axis_index("ctx")
    local_x = sequence[0]
    local_rows, model_width = local_x.shape
    own_rows = local_rows // exp_count
    length = local_rows * ctx_count
    normed = rms_scale(local_x, norm1_gain)
    projected = jnp.einsum("ti,igd->tgd", normed, w_in, preferred_element_type=jnp.float32)
    source = projected[:, 1] * projected[:, 0]
    positions = (ctx_pos * local_rows + jnp.arange(local_rows, dtype=jnp.int32)).astype(jnp.float32)
    shaped = long_filter * jnp.exp(-filter_decay[None, :] * positions[:, None] / length)
    convolved = causal_convolve(source, shaped)
    gated_rows = (projected[:, 2] * (convolved + conv_bias[None, :] * source)).astype(jnp.bfloat16)
    mixed_full = jnp.dot(gated_rows, w_out, preferred_element_type=jnp.float32)
    mixed_sum = a2a_reduce(mixed_full, "exp", jnp.bfloat16)
    residual_rows = lax.dynamic_slice_in_dim(local_x, exp_pos * own_rows, own_rows, 0)
    hidden_state = stored(residual_rows.astype(jnp.float32) + mixed_sum)
    routed_in = rms_scale(hidden_state, norm2_gain)
    chances = jax.nn.sigmoid(jnp.dot(routed_in, router, preferred_element_type=jnp.float32))
    picked_ids = experts[0]
    slot_ids = expert_slots[0]
    chosen = jnp.take_along_axis(chances, picked_ids, axis=1)
    weights = chosen / jnp.sum(chosen, axis=1, keepdims=True)
    n_experts = router.shape[1]
    capacity = 4 * own_rows // exp_count
    slot_rows = picked_ids * capacity + slot_ids
    buffer_ids = jnp.arange(n_experts * capacity, dtype=jnp.int32)[:, None]
    selector = (
        (slot_rows[None, :, 0] == buffer_ids) | (slot_rows[None, :, 1] == buffer_ids)
    ).astype(jnp.bfloat16)
    outgoing = jnp.dot(selector, routed_in, preferred_element_type=jnp.float32).astype(jnp.bfloat16)
    outgoing = outgoing.reshape(n_experts, capacity, model_width)
    gate_local = w_gate[0]
    up_local = w_up[0]
    down_local = w_down[0]
    copies = jnp.broadcast_to(outgoing[None], (ctx_count, n_experts, capacity, model_width))
    arrived = token_move(copies.reshape(ctx_count * n_experts, capacity, model_width))
    token_rows = arrived.reshape(-1, model_width)
    gate_val = jnp.dot(token_rows, gate_local, preferred_element_type=jnp.float32)
    up_val = jnp.dot(token_rows, up_local, preferred_element_type=jnp.float32)
    slice_hidden = lax.optimization_barrier((jax.nn.silu(gate_val) * up_val).astype(jnp.bfloat16))
    slice_part = (
        jnp.dot(slice_hidden, down_local, preferred_element_type=jnp.float32)
        .astype(jnp.bfloat16)
        .reshape(ctx_count * n_experts, capacity, model_width)
    )
    came_back = token_move(slice_part)
    summed = jnp.sum(
        came_back.reshape(ctx_count, n_experts, capacity, model_width).astype(jnp.float32), axis=0
    )
    expert_out = stored(summed)
    flat_out = expert_out.reshape(n_experts * capacity, model_width)
    first_rows = jnp.take(flat_out, slot_rows[:, 0], axis=0).astype(jnp.float32)
    second_rows = jnp.take(flat_out, slot_rows[:, 1], axis=0).astype(jnp.float32)
    combined = weights[:, 0:1] * first_rows + weights[:, 1:2] * second_rows
    block_final = stored(hidden_state.astype(jnp.float32) + combined)
    usage_prob = jax.nn.sigmoid(
        jnp.einsum("td,od->to", block_final, splice_head, preferred_element_type=jnp.float32)
    )
    all_tokens = lax.axis_size("rep") * ctx_count * exp_count * own_rows
    loss_scale = 1.0 / math.sqrt(all_tokens)
    usage_grad = ((usage_prob - targets[0]) * loss_scale).astype(jnp.bfloat16)
    local_grad = jnp.einsum(
        "td,to->do", block_final, usage_grad, preferred_element_type=jnp.float32
    )
    head_total = a2a_allreduce(local_grad, ("ctx", "exp", "rep"), jnp.bfloat16).T
    return (block_final[None], head_total)


def solution(mesh):
    in_specs = (
        P("rep", "ctx", None),
        P(),
        P(None, None, "exp"),
        P("ctx", "exp"),
        P("exp"),
        P("exp"),
        P("exp", None),
        P(),
        P(),
        P("exp", None, "ctx"),
        P("exp", None, "ctx"),
        P("exp", "ctx", None),
        P("rep", ("ctx", "exp"), None),
        P("rep", ("ctx", "exp"), None),
        P(),
        P("rep", ("ctx", "exp"), None),
    )
    out_specs = (P("rep", ("ctx", "exp"), None), P())
    return jax.shard_map(shards, mesh=mesh, in_specs=in_specs, out_specs=out_specs, check_vma=False)
```

```python
import math

import jax
import jax.numpy as jnp
from jax import lax
from jax.sharding import PartitionSpec as P

TWO_PI = 2.0 * math.pi


def stored(values):
    return lax.optimization_barrier(values.astype(jnp.bfloat16))


def rms_scale(token_rows, norm_gain):
    wide = token_rows.astype(jnp.float32)
    inverse = lax.rsqrt(jnp.mean(wide * wide, axis=-1, keepdims=True) + 1e-05)
    return (wide * inverse * norm_gain).astype(jnp.bfloat16)


def phase_table(first_ids, second_ids, modulus):
    angle = (
        TWO_PI * (first_ids[:, None] * second_ids[None, :] % modulus).astype(jnp.float32) / modulus
    )
    return (jnp.cos(angle), jnp.sin(angle))


def spectra_move(blocks):
    return lax.all_to_all(blocks, "ctx", split_axis=0, concat_axis=1, tiled=True)


def a2a_reduce(values, axes, wire=None):
    count = lax.axis_size(axes)
    sent = values.reshape((count, -1) + values.shape[1:])
    if wire is not None:
        sent = sent.astype(wire)
    pieces = lax.all_to_all(sent, axes, 0, 0, tiled=True)
    return jnp.sum(pieces.astype(jnp.float32), axis=0)


def a2a_allreduce(values, axes, wire=None):
    count = lax.axis_size(axes)
    if values.shape[0] % count:
        return lax.psum(values, axes)
    mine = a2a_reduce(values, axes, wire)
    if wire is not None:
        mine = mine.astype(wire)
    spread = jnp.broadcast_to(mine[None], (count,) + mine.shape)
    gathered = lax.all_to_all(spread, axes, 0, 0, tiled=True)
    return gathered.astype(jnp.float32).reshape(values.shape)


def token_move(blocks):
    return lax.all_to_all(blocks, ("ctx", "exp"), split_axis=0, concat_axis=0, tiled=True)


def local_convolve(whole):
    highest = lax.Precision.HIGHEST
    _, lanes, length = whole.shape
    points = 2 * length
    outer = int(round(math.sqrt(points)))
    while points % outer:
        outer -= 1
    inner = points // outer
    half = length // inner
    rows = whole.reshape(2 * lanes, half, inner)
    a_ids = jnp.arange(half, dtype=jnp.int32)
    k1_ids = jnp.arange(outer, dtype=jnp.int32)
    b_ids = jnp.arange(inner, dtype=jnp.int32)
    k2_ids = jnp.arange(points // inner, dtype=jnp.int32)
    cos_first, sin_first = phase_table(a_ids, k1_ids, outer)
    cos_twist, sin_twist = phase_table(k1_ids, b_ids, points)
    cos_last, sin_last = phase_table(b_ids, k2_ids, inner)
    a_re = jnp.einsum("cab,ak->ckb", rows, cos_first, precision=highest)
    a_im = -jnp.einsum("cab,ak->ckb", rows, sin_first, precision=highest)
    b_re = a_re * cos_twist + a_im * sin_twist
    b_im = a_im * cos_twist - a_re * sin_twist
    x_re = jnp.einsum("ckb,bj->ckj", b_re, cos_last, precision=highest) + jnp.einsum(
        "ckb,bj->ckj", b_im, sin_last, precision=highest
    )
    x_im = jnp.einsum("ckb,bj->ckj", b_im, cos_last, precision=highest) - jnp.einsum(
        "ckb,bj->ckj", b_re, sin_last, precision=highest
    )
    p_re = x_re[:lanes] * x_re[lanes:] - x_im[:lanes] * x_im[lanes:]
    p_im = x_re[:lanes] * x_im[lanes:] + x_im[:lanes] * x_re[lanes:]
    c_re = jnp.einsum("ckj,mj->ckm", p_re, cos_last, precision=highest) - jnp.einsum(
        "ckj,mj->ckm", p_im, sin_last, precision=highest
    )
    c_im = jnp.einsum("ckj,mj->ckm", p_im, cos_last, precision=highest) + jnp.einsum(
        "ckj,mj->ckm", p_re, sin_last, precision=highest
    )
    d_re = c_re * cos_twist - c_im * sin_twist
    d_im = c_im * cos_twist + c_re * sin_twist
    out = jnp.einsum("ckm,lk->clm", d_re, cos_first, precision=highest) - jnp.einsum(
        "ckm,lk->clm", d_im, sin_first, precision=highest
    )
    return out.reshape(lanes, length) / points


def causal_convolve(source, shaped):
    both = jnp.stack([source, shaped], axis=0)
    whole = lax.all_to_all(both, "ctx", split_axis=1, concat_axis=2, tiled=True)
    convolved = local_convolve(whole)
    return lax.all_to_all(convolved, "ctx", split_axis=1, concat_axis=0, tiled=True)


def shards(
    sequence,
    norm1_gain,
    w_in,
    long_filter,
    filter_decay,
    conv_bias,
    w_out,
    norm2_gain,
    router,
    w_gate,
    w_up,
    w_down,
    experts,
    expert_slots,
    splice_head,
    targets,
):
    exp_count = lax.axis_size("exp")
    exp_pos = lax.axis_index("exp")
    ctx_count = lax.axis_size("ctx")
    ctx_pos = lax.axis_index("ctx")
    local_x = sequence[0]
    local_rows, model_width = local_x.shape
    own_rows = local_rows // exp_count
    length = local_rows * ctx_count
    normed = rms_scale(local_x, norm1_gain)
    projected = jnp.einsum("ti,igd->gdt", normed, w_in, preferred_element_type=jnp.float32)
    source = projected[1] * projected[0]
    positions = (ctx_pos * local_rows + jnp.arange(local_rows, dtype=jnp.int32)).astype(jnp.float32)
    shaped = long_filter.T * jnp.exp(-filter_decay[:, None] * positions[None, :] / length)
    convolved = causal_convolve(source, shaped)
    gated_rows = (projected[2] * (convolved + conv_bias[:, None] * source)).astype(jnp.bfloat16)
    mixed_full = jnp.einsum("dt,de->te", gated_rows, w_out, preferred_element_type=jnp.float32)
    mixed_sum = a2a_reduce(mixed_full, "exp", jnp.bfloat16)
    residual_rows = lax.dynamic_slice_in_dim(local_x, exp_pos * own_rows, own_rows, 0)
    hidden_state = stored(residual_rows.astype(jnp.float32) + mixed_sum)
    routed_in = rms_scale(hidden_state, norm2_gain)
    chances = jax.nn.sigmoid(jnp.dot(routed_in, router, preferred_element_type=jnp.float32))
    picked_ids = experts[0]
    slot_ids = expert_slots[0]
    chosen = jnp.take_along_axis(chances, picked_ids, axis=1)
    weights = chosen / jnp.sum(chosen, axis=1, keepdims=True)
    n_experts = router.shape[1]
    capacity = 4 * own_rows // exp_count
    slot_rows = picked_ids * capacity + slot_ids
    buffer_ids = jnp.arange(n_experts * capacity, dtype=jnp.int32)[:, None]
    selector = (
        (slot_rows[None, :, 0] == buffer_ids) | (slot_rows[None, :, 1] == buffer_ids)
    ).astype(jnp.bfloat16)
    outgoing = jnp.dot(selector, routed_in, preferred_element_type=jnp.float32).astype(jnp.bfloat16)
    outgoing = outgoing.reshape(n_experts, capacity, model_width)
    gate_local = w_gate[0]
    up_local = w_up[0]
    down_local = w_down[0]
    copies = jnp.broadcast_to(outgoing[None], (ctx_count, n_experts, capacity, model_width))
    arrived = token_move(copies.reshape(ctx_count * n_experts, capacity, model_width))
    token_rows = arrived.reshape(-1, model_width)
    gate_val = jnp.dot(token_rows, gate_local, preferred_element_type=jnp.float32)
    up_val = jnp.dot(token_rows, up_local, preferred_element_type=jnp.float32)
    slice_hidden = lax.optimization_barrier((jax.nn.silu(gate_val) * up_val).astype(jnp.bfloat16))
    slice_part = (
        jnp.dot(slice_hidden, down_local, preferred_element_type=jnp.float32)
        .astype(jnp.bfloat16)
        .reshape(ctx_count * n_experts, capacity, model_width)
    )
    came_back = token_move(slice_part)
    summed = jnp.sum(
        came_back.reshape(ctx_count, n_experts, capacity, model_width).astype(jnp.float32), axis=0
    )
    expert_out = stored(summed)
    flat_out = expert_out.reshape(n_experts * capacity, model_width)
    first_rows = jnp.take(flat_out, slot_rows[:, 0], axis=0).astype(jnp.float32)
    second_rows = jnp.take(flat_out, slot_rows[:, 1], axis=0).astype(jnp.float32)
    combined = weights[:, 0:1] * first_rows + weights[:, 1:2] * second_rows
    block_final = stored(hidden_state.astype(jnp.float32) + combined)
    usage_prob = jax.nn.sigmoid(
        jnp.einsum("td,od->to", block_final, splice_head, preferred_element_type=jnp.float32)
    )
    all_tokens = lax.axis_size("rep") * ctx_count * exp_count * own_rows
    loss_scale = 1.0 / math.sqrt(all_tokens)
    usage_grad = ((usage_prob - targets[0]) * loss_scale).astype(jnp.bfloat16)
    local_grad = jnp.einsum(
        "td,to->do", block_final, usage_grad, preferred_element_type=jnp.float32
    )
    head_total = a2a_allreduce(local_grad, ("ctx", "exp", "rep"), jnp.bfloat16).T
    return (block_final[None], head_total)


def solution(mesh):
    in_specs = (
        P("rep", "ctx", None),
        P(),
        P(None, None, "exp"),
        P("ctx", "exp"),
        P("exp"),
        P("exp"),
        P("exp", None),
        P(),
        P(),
        P("exp", None, "ctx"),
        P("exp", None, "ctx"),
        P("exp", "ctx", None),
        P("rep", ("ctx", "exp"), None),
        P("rep", ("ctx", "exp"), None),
        P(),
        P("rep", ("ctx", "exp"), None),
    )
    out_specs = (P("rep", ("ctx", "exp"), None), P())
    return jax.shard_map(shards, mesh=mesh, in_specs=in_specs, out_specs=out_specs, check_vma=False)
```

```python
import math

import jax
import jax.numpy as jnp
from jax import lax
from jax.sharding import PartitionSpec as P

TWO_PI = 2.0 * math.pi


def stored(values):
    return lax.optimization_barrier(values.astype(jnp.bfloat16))


def rms_scale(token_rows, norm_gain):
    wide = token_rows.astype(jnp.float32)
    inverse = lax.rsqrt(jnp.mean(wide * wide, axis=-1, keepdims=True) + 1e-05)
    return (wide * inverse * norm_gain).astype(jnp.bfloat16)


def phase_table(first_ids, second_ids, modulus):
    angle = (
        TWO_PI * (first_ids[:, None] * second_ids[None, :] % modulus).astype(jnp.float32) / modulus
    )
    return (jnp.cos(angle), jnp.sin(angle))


def spectra_move(blocks):
    return lax.all_to_all(blocks, "ctx", split_axis=0, concat_axis=1, tiled=True)


def a2a_reduce(values, axes, wire=None):
    count = lax.axis_size(axes)
    sent = values.reshape((count, -1) + values.shape[1:])
    if wire is not None:
        sent = sent.astype(wire)
    pieces = lax.all_to_all(sent, axes, 0, 0, tiled=True)
    return jnp.sum(pieces.astype(jnp.float32), axis=0)


def a2a_allreduce(values, axes, wire=None):
    count = lax.axis_size(axes)
    if values.shape[0] % count:
        return lax.psum(values, axes)
    mine = a2a_reduce(values, axes, wire)
    if wire is not None:
        mine = mine.astype(wire)
    spread = jnp.broadcast_to(mine[None], (count,) + mine.shape)
    gathered = lax.all_to_all(spread, axes, 0, 0, tiled=True)
    return gathered.astype(jnp.float32).reshape(values.shape)


def token_move(blocks):
    return lax.all_to_all(blocks, ("ctx", "exp"), split_axis=0, concat_axis=0, tiled=True)


def local_convolve(whole):
    highest = lax.Precision.HIGHEST
    _, lanes, length = whole.shape
    points = 2 * length
    outer = int(round(math.sqrt(points)))
    while points % outer:
        outer -= 1
    inner = points // outer
    half = length // inner
    rows = whole.reshape(2 * lanes, half, inner)
    a_ids = jnp.arange(half, dtype=jnp.int32)
    k1_ids = jnp.arange(outer, dtype=jnp.int32)
    b_ids = jnp.arange(inner, dtype=jnp.int32)
    k2_ids = jnp.arange(points // inner, dtype=jnp.int32)
    cos_first, sin_first = phase_table(a_ids, k1_ids, outer)
    cos_twist, sin_twist = phase_table(k1_ids, b_ids, points)
    cos_last, sin_last = phase_table(b_ids, k2_ids, inner)
    a_re = jnp.einsum("cab,ak->ckb", rows, cos_first, precision=highest)
    a_im = -jnp.einsum("cab,ak->ckb", rows, sin_first, precision=highest)
    b_re = a_re * cos_twist + a_im * sin_twist
    b_im = a_im * cos_twist - a_re * sin_twist
    x_re = jnp.einsum("ckb,bj->ckj", b_re, cos_last, precision=highest) + jnp.einsum(
        "ckb,bj->ckj", b_im, sin_last, precision=highest
    )
    x_im = jnp.einsum("ckb,bj->ckj", b_im, cos_last, precision=highest) - jnp.einsum(
        "ckb,bj->ckj", b_re, sin_last, precision=highest
    )
    p_re = x_re[:lanes] * x_re[lanes:] - x_im[:lanes] * x_im[lanes:]
    p_im = x_re[:lanes] * x_im[lanes:] + x_im[:lanes] * x_re[lanes:]
    c_re = jnp.einsum("ckj,mj->ckm", p_re, cos_last, precision=highest) - jnp.einsum(
        "ckj,mj->ckm", p_im, sin_last, precision=highest
    )
    c_im = jnp.einsum("ckj,mj->ckm", p_im, cos_last, precision=highest) + jnp.einsum(
        "ckj,mj->ckm", p_re, sin_last, precision=highest
    )
    d_re = c_re * cos_twist - c_im * sin_twist
    d_im = c_im * cos_twist + c_re * sin_twist
    out = jnp.einsum("ckm,lk->clm", d_re, cos_first, precision=highest) - jnp.einsum(
        "ckm,lk->clm", d_im, sin_first, precision=highest
    )
    return out.reshape(lanes, length) / points


def causal_convolve(source, shaped):
    both = jnp.stack([source.T, shaped.T], axis=0)
    whole = lax.all_to_all(both, "ctx", split_axis=1, concat_axis=2, tiled=True)
    convolved = local_convolve(whole)
    back = lax.all_to_all(convolved, "ctx", split_axis=1, concat_axis=0, tiled=True)
    return back.T


def shards(
    sequence,
    norm1_gain,
    w_in,
    long_filter,
    filter_decay,
    conv_bias,
    w_out,
    norm2_gain,
    router,
    w_gate,
    w_up,
    w_down,
    experts,
    expert_slots,
    splice_head,
    targets,
):
    exp_count = lax.axis_size("exp")
    exp_pos = lax.axis_index("exp")
    ctx_count = lax.axis_size("ctx")
    ctx_pos = lax.axis_index("ctx")
    local_x = sequence[0]
    local_rows, model_width = local_x.shape
    own_rows = local_rows // exp_count
    length = local_rows * ctx_count
    normed = rms_scale(local_x, norm1_gain)
    projected = jnp.einsum("ti,igd->tgd", normed, w_in, preferred_element_type=jnp.float32)
    source = projected[:, 1] * projected[:, 0]
    positions = (ctx_pos * local_rows + jnp.arange(local_rows, dtype=jnp.int32)).astype(jnp.float32)
    shaped = long_filter * jnp.exp(-filter_decay[None, :] * positions[:, None] / length)
    convolved = causal_convolve(source, shaped)
    gated_rows = (projected[:, 2] * (convolved + conv_bias[None, :] * source)).astype(jnp.bfloat16)
    mixed_full = jnp.dot(gated_rows, w_out, preferred_element_type=jnp.float32)
    mixed_sum = a2a_reduce(mixed_full, "exp", jnp.bfloat16)
    residual_rows = lax.dynamic_slice_in_dim(local_x, exp_pos * own_rows, own_rows, 0)
    hidden_state = stored(residual_rows.astype(jnp.float32) + mixed_sum)
    routed_in = rms_scale(hidden_state, norm2_gain)
    chances = jax.nn.sigmoid(jnp.dot(routed_in, router, preferred_element_type=jnp.float32))
    picked_ids = experts[0]
    slot_ids = expert_slots[0]
    chosen = jnp.take_along_axis(chances, picked_ids, axis=1)
    weights = chosen / jnp.sum(chosen, axis=1, keepdims=True)
    n_experts = router.shape[1]
    capacity = 4 * own_rows // exp_count
    slot_rows = picked_ids * capacity + slot_ids
    buffer_ids = jnp.arange(n_experts * capacity, dtype=jnp.int32)[:, None]
    selector = (
        (slot_rows[None, :, 0] == buffer_ids) | (slot_rows[None, :, 1] == buffer_ids)
    ).astype(jnp.bfloat16)
    outgoing = jnp.dot(selector, routed_in, preferred_element_type=jnp.float32).astype(jnp.bfloat16)
    outgoing = outgoing.reshape(n_experts, capacity, model_width)
    gate_local = w_gate[0]
    up_local = w_up[0]
    down_local = w_down[0]
    copies = jnp.broadcast_to(outgoing[None], (ctx_count, n_experts, capacity, model_width))
    arrived = token_move(copies.reshape(ctx_count * n_experts, capacity, model_width))
    token_rows = arrived.reshape(-1, model_width)
    gate_val = jnp.dot(token_rows, gate_local, preferred_element_type=jnp.float32)
    up_val = jnp.dot(token_rows, up_local, preferred_element_type=jnp.float32)
    slice_hidden = lax.optimization_barrier((jax.nn.silu(gate_val) * up_val).astype(jnp.bfloat16))
    slice_part = (
        jnp.dot(slice_hidden, down_local, preferred_element_type=jnp.float32)
        .astype(jnp.bfloat16)
        .reshape(ctx_count * n_experts, capacity, model_width)
    )
    came_back = token_move(slice_part)
    summed = jnp.sum(
        came_back.reshape(ctx_count, n_experts, capacity, model_width).astype(jnp.float32), axis=0
    )
    expert_out = stored(summed)
    flat_out = expert_out.reshape(n_experts * capacity, model_width)
    first_rows = jnp.take(flat_out, slot_rows[:, 0], axis=0).astype(jnp.float32)
    second_rows = jnp.take(flat_out, slot_rows[:, 1], axis=0).astype(jnp.float32)
    combined = weights[:, 0:1] * first_rows + weights[:, 1:2] * second_rows
    block_final = stored(hidden_state.astype(jnp.float32) + combined)
    usage_prob = jax.nn.sigmoid(
        jnp.einsum("td,od->to", block_final, splice_head, preferred_element_type=jnp.float32)
    )
    all_tokens = lax.axis_size("rep") * ctx_count * exp_count * own_rows
    loss_scale = 1.0 / math.sqrt(all_tokens)
    usage_grad = ((usage_prob - targets[0]) * loss_scale).astype(jnp.bfloat16)
    local_grad = jnp.einsum(
        "td,to->do", block_final, usage_grad, preferred_element_type=jnp.bfloat16
    )
    head_total = a2a_allreduce(local_grad, ("ctx", "exp", "rep"), jnp.bfloat16).T
    return (block_final[None], head_total)


def solution(mesh):
    in_specs = (
        P("rep", "ctx", None),
        P(),
        P(None, None, "exp"),
        P("ctx", "exp"),
        P("exp"),
        P("exp"),
        P("exp", None),
        P(),
        P(),
        P("exp", None, "ctx"),
        P("exp", None, "ctx"),
        P("exp", "ctx", None),
        P("rep", ("ctx", "exp"), None),
        P("rep", ("ctx", "exp"), None),
        P(),
        P("rep", ("ctx", "exp"), None),
    )
    out_specs = (P("rep", ("ctx", "exp"), None), P())
    return jax.shard_map(shards, mesh=mesh, in_specs=in_specs, out_specs=out_specs, check_vma=False)
```

```python
import math

import jax
import jax.numpy as jnp
from jax import lax
from jax.sharding import PartitionSpec as P

TWO_PI = 2.0 * math.pi


def stored(values):
    return lax.optimization_barrier(values.astype(jnp.bfloat16))


def rms_scale(token_rows, norm_gain):
    wide = token_rows.astype(jnp.float32)
    inverse = lax.rsqrt(jnp.mean(wide * wide, axis=-1, keepdims=True) + 1e-05)
    return (wide * inverse * norm_gain).astype(jnp.bfloat16)


def phase_table(first_ids, second_ids, modulus):
    angle = (
        TWO_PI * (first_ids[:, None] * second_ids[None, :] % modulus).astype(jnp.float32) / modulus
    )
    return (jnp.cos(angle), jnp.sin(angle))


def spectra_move(blocks):
    return lax.all_to_all(blocks, "ctx", split_axis=0, concat_axis=1, tiled=True)


def a2a_reduce(values, axes, wire=None):
    count = lax.axis_size(axes)
    sent = values.reshape((count, -1) + values.shape[1:])
    if wire is not None:
        sent = sent.astype(wire)
    pieces = lax.all_to_all(sent, axes, 0, 0, tiled=True)
    return jnp.sum(pieces.astype(jnp.float32), axis=0)


def a2a_allreduce(values, axes, wire=None):
    count = lax.axis_size(axes)
    if values.shape[0] % count:
        return lax.psum(values, axes)
    mine = a2a_reduce(values, axes, wire)
    if wire is not None:
        mine = mine.astype(wire)
    spread = jnp.broadcast_to(mine[None], (count,) + mine.shape)
    gathered = lax.all_to_all(spread, axes, 0, 0, tiled=True)
    return gathered.astype(jnp.float32).reshape(values.shape)


def token_move(blocks):
    return lax.all_to_all(blocks, ("ctx", "exp"), split_axis=0, concat_axis=0, tiled=True)


def local_convolve(whole):
    highest = lax.Precision.HIGHEST
    _, lanes, length = whole.shape
    points = 2 * length
    outer = int(round(math.sqrt(points)))
    while points % outer:
        outer -= 1
    inner = points // outer
    half = length // inner
    rows = whole.reshape(2 * lanes, half, inner)
    a_ids = jnp.arange(half, dtype=jnp.int32)
    k1_ids = jnp.arange(outer, dtype=jnp.int32)
    b_ids = jnp.arange(inner, dtype=jnp.int32)
    k2_ids = jnp.arange(points // inner, dtype=jnp.int32)
    cos_first, sin_first = phase_table(a_ids, k1_ids, outer)
    cos_twist, sin_twist = phase_table(k1_ids, b_ids, points)
    cos_last, sin_last = phase_table(b_ids, k2_ids, inner)
    a_re = jnp.einsum("cab,ak->ckb", rows, cos_first, precision=highest)
    a_im = -jnp.einsum("cab,ak->ckb", rows, sin_first, precision=highest)
    b_re = a_re * cos_twist + a_im * sin_twist
    b_im = a_im * cos_twist - a_re * sin_twist
    x_re = jnp.einsum("ckb,bj->ckj", b_re, cos_last, precision=highest) + jnp.einsum(
        "ckb,bj->ckj", b_im, sin_last, precision=highest
    )
    x_im = jnp.einsum("ckb,bj->ckj", b_im, cos_last, precision=highest) - jnp.einsum(
        "ckb,bj->ckj", b_re, sin_last, precision=highest
    )
    p_re = x_re[:lanes] * x_re[lanes:] - x_im[:lanes] * x_im[lanes:]
    p_im = x_re[:lanes] * x_im[lanes:] + x_im[:lanes] * x_re[lanes:]
    c_re = jnp.einsum("ckj,mj->ckm", p_re, cos_last, precision=highest) - jnp.einsum(
        "ckj,mj->ckm", p_im, sin_last, precision=highest
    )
    c_im = jnp.einsum("ckj,mj->ckm", p_im, cos_last, precision=highest) + jnp.einsum(
        "ckj,mj->ckm", p_re, sin_last, precision=highest
    )
    d_re = c_re * cos_twist - c_im * sin_twist
    d_im = c_im * cos_twist + c_re * sin_twist
    out = jnp.einsum("ckm,lk->clm", d_re, cos_first, precision=highest) - jnp.einsum(
        "ckm,lk->clm", d_im, sin_first, precision=highest
    )
    return out.reshape(lanes, length) / points


def causal_convolve(source, shaped):
    both = jnp.stack([source.T, shaped.T], axis=0)
    whole = lax.all_to_all(both, "ctx", split_axis=1, concat_axis=2, tiled=True)
    convolved = local_convolve(whole)
    back = lax.all_to_all(convolved, "ctx", split_axis=1, concat_axis=0, tiled=True)
    return back.T


def shards(
    sequence,
    norm1_gain,
    w_in,
    long_filter,
    filter_decay,
    conv_bias,
    w_out,
    norm2_gain,
    router,
    w_gate,
    w_up,
    w_down,
    experts,
    expert_slots,
    splice_head,
    targets,
):
    exp_count = lax.axis_size("exp")
    exp_pos = lax.axis_index("exp")
    ctx_count = lax.axis_size("ctx")
    ctx_pos = lax.axis_index("ctx")
    local_x = sequence[0]
    local_rows, model_width = local_x.shape
    own_rows = local_rows // exp_count
    length = local_rows * ctx_count
    normed = rms_scale(local_x, norm1_gain)
    projected = jnp.einsum("ti,igd->tgd", normed, w_in, preferred_element_type=jnp.float32)
    source = projected[:, 1] * projected[:, 0]
    positions = (ctx_pos * local_rows + jnp.arange(local_rows, dtype=jnp.int32)).astype(jnp.float32)
    shaped = long_filter * jnp.exp(-filter_decay[None, :] * positions[:, None] / length)
    convolved = causal_convolve(source, shaped)
    gated_rows = (projected[:, 2] * (convolved + conv_bias[None, :] * source)).astype(jnp.bfloat16)
    mixed_full = jnp.dot(gated_rows, w_out, preferred_element_type=jnp.float32)
    mixed_sum = a2a_reduce(mixed_full, "exp", jnp.bfloat16)
    residual_rows = lax.dynamic_slice_in_dim(local_x, exp_pos * own_rows, own_rows, 0)
    hidden_state = stored(residual_rows.astype(jnp.float32) + mixed_sum)
    routed_in = rms_scale(hidden_state, norm2_gain)
    chances = jax.nn.sigmoid(jnp.dot(routed_in, router, preferred_element_type=jnp.float32))
    picked_ids = experts[0]
    slot_ids = expert_slots[0]
    chosen = jnp.take_along_axis(chances, picked_ids, axis=1)
    weights = chosen / jnp.sum(chosen, axis=1, keepdims=True)
    n_experts = router.shape[1]
    capacity = 4 * own_rows // exp_count
    slot_rows = picked_ids * capacity + slot_ids
    buffer_ids = jnp.arange(n_experts * capacity, dtype=jnp.int32)[:, None]
    selector = (
        (slot_rows[None, :, 0] == buffer_ids) | (slot_rows[None, :, 1] == buffer_ids)
    ).astype(jnp.bfloat16)
    outgoing = jnp.dot(selector, routed_in, preferred_element_type=jnp.float32).astype(jnp.bfloat16)
    outgoing = outgoing.reshape(n_experts, capacity, model_width)
    gate_local = w_gate[0]
    up_local = w_up[0]
    down_local = w_down[0]
    copies = jnp.broadcast_to(outgoing[None], (ctx_count, n_experts, capacity, model_width))
    arrived = token_move(copies.reshape(ctx_count * n_experts, capacity, model_width))
    token_rows = arrived.reshape(-1, model_width)
    gate_val = jnp.dot(token_rows, gate_local, preferred_element_type=jnp.float32)
    up_val = jnp.dot(token_rows, up_local, preferred_element_type=jnp.float32)
    slice_hidden = lax.optimization_barrier((jax.nn.silu(gate_val) * up_val).astype(jnp.bfloat16))
    slice_part = (
        jnp.dot(slice_hidden, down_local, preferred_element_type=jnp.float32)
        .astype(jnp.bfloat16)
        .reshape(ctx_count * n_experts, capacity, model_width)
    )
    came_back = token_move(slice_part)
    summed = jnp.sum(
        came_back.reshape(ctx_count, n_experts, capacity, model_width).astype(jnp.float32), axis=0
    )
    expert_out = stored(summed)
    flat_out = expert_out.reshape(n_experts * capacity, model_width)
    first_rows = jnp.take(flat_out, slot_rows[:, 0], axis=0).astype(jnp.float32)
    second_rows = jnp.take(flat_out, slot_rows[:, 1], axis=0).astype(jnp.float32)
    combined = weights[:, 0:1] * first_rows + weights[:, 1:2] * second_rows
    block_final = stored(hidden_state.astype(jnp.float32) + combined)
    usage_prob = jax.nn.sigmoid(
        jnp.einsum("td,od->to", block_final, splice_head, preferred_element_type=jnp.float32)
    )
    all_tokens = lax.axis_size("rep") * ctx_count * exp_count * own_rows
    loss_scale = 1.0 / math.sqrt(all_tokens)
    usage_grad = ((usage_prob - targets[0]) * loss_scale).astype(jnp.bfloat16)
    local_grad = jnp.einsum(
        "td,to->do", block_final, usage_grad, preferred_element_type=jnp.bfloat16
    )
    head_total = a2a_allreduce(local_grad, ("exp", "ctx", "rep"), jnp.bfloat16).T
    return (block_final[None], head_total)


def solution(mesh):
    in_specs = (
        P("rep", "ctx", None),
        P(),
        P(None, None, "exp"),
        P("ctx", "exp"),
        P("exp"),
        P("exp"),
        P("exp", None),
        P(),
        P(),
        P("exp", None, "ctx"),
        P("exp", None, "ctx"),
        P("exp", "ctx", None),
        P("rep", ("ctx", "exp"), None),
        P("rep", ("ctx", "exp"), None),
        P(),
        P("rep", ("ctx", "exp"), None),
    )
    out_specs = (P("rep", ("ctx", "exp"), None), P())
    return jax.shard_map(shards, mesh=mesh, in_specs=in_specs, out_specs=out_specs, check_vma=False)
```
